512 devices in a mesh: gx: 32 (over z_hi, x, core), gy: 4 (over y), gz: 4 (over z_lo).
Axes of the slice: x: 4, y: 4, z: 16 (z_hi: 4, z_lo: 4; z = z_hi * 4 + z_lo), core: 2. Of those that a mesh axis runs over, the one named last changes fastest.
Arguments:
- level_set: float32 [1024, 128, 512], P('gx', 'gy', 'gz'), may hold values from -6 to 6
- velocity: bfloat16 [3, 1024, 128, 512], P(None, 'gx', 'gy', 'gz'), may hold values from -1 to 1
- active_brick: int32 [32, 4, 4], P('gx', 'gy', 'gz'), may hold values 0 or 1
- depth_order: int32 [4], replicated, may hold values from 0 to 3, as said below
Outputs:
- level_out: float32 [1024, 128, 512], P('gx', 'gy', 'gz')
- image: float32 [4, 2048, 256], P(None, ('gx', 'gz'), 'gy')
The draws below stay inside these ranges and needn't reach their ends.
Inputs may be any that keep to these rules, and one draw needn't show every extreme that they name: `depth_order`: either 0, 1, .. in slab order or the reverse.
All inputs are finite; a program needn't handle non-finite values. No bound on the sum of `active_brick` on one device may be relied on, other than what follows from the above.
Results may differ from the reference program's by a relative error of at most 0.0003.
Values may be sent and summed in bfloat16 or wider, within the bound.
No kernel may reach another device: no remote copies, remote signals or barrier semaphores. Data moves between devices by JAX's collectives and lax.ppermute only.
A program may use at most 64 MiB of HBM per device.

```python
import jax
import jax.numpy as jnp
from jax import lax

CX = 32
CY = 32
CZ = 128
NX = 1024
NY = 128
NZ = 512
N_GX = 32
N_GY = 4
N_GZ = 4


def draw_depth_order(key, part):
    flipped = jax.random.randint(key, (), 0, 2)
    ranks = jnp.arange(N_GZ, dtype=jnp.int32)
    return jnp.where(flipped == 1, N_GZ - 1 - ranks, ranks).astype(jnp.int32)


def touch_ends(drawn, key, least, largest):
    index_at = [jax.random.randint(jax.random.fold_in(key, axis), (), 0, length) for axis, length in enumerate(drawn.shape)]
    widest = drawn.shape.index(max(drawn.shape))
    next_to = index_at[:widest] + [(index_at[widest] + 1) % drawn.shape[widest]] + index_at[widest + 1:]
    return drawn.at[tuple(index_at)].set(least).at[tuple(next_to)].set(largest)


def block_levels(key, shape, split, least, high):
    gain = 1.0
    for axis_at, shards_of in split:
        draws = jax.random.uniform(jax.random.fold_in(jax.random.fold_in(key, 6), axis_at), (shards_of,), jnp.float32, least / len(split), high / len(split))
        gain = gain * jnp.repeat(jnp.exp(draws), shape[axis_at] // shards_of).reshape((-1,) + (1,) * (len(shape) - 1 - axis_at))
    return gain


def scatter_about(key, dims, width, most, pieces=(), held_as=jnp.bfloat16):
    drawn = width * jax.random.normal(key, dims, jnp.float32)
    if pieces:
        drawn = drawn * block_levels(key, dims, pieces, -0.22, 0.18)
    return jnp.clip(drawn, -most, most).astype(held_as)


def setup_inputs(seed: int = 0) -> dict:
    splits = jax.random.split(jax.random.key(seed), 5)
    return {
        "level_set": scatter_about(splits[0], (NX, NY, NZ), 1.0, 6.0, ((0, 32), (1, 4), (2, 4)), jnp.float32),
        "velocity": jnp.clip(jax.random.uniform(splits[1], (3, NX, NY, NZ), jnp.float32, -1.0, 1.0) * block_levels(splits[1], (3, NX, NY, NZ), ((1, 32), (2, 4), (3, 4)), -0.4, 0.0), -1.0, 1.0).astype(jnp.bfloat16),
        "active_brick": touch_ends((jax.random.randint(splits[2], (N_GX, N_GY, N_GZ), 0, 4) < 3).astype(jnp.int32), jax.random.fold_in(splits[2], 1), 0, 1),
        "depth_order": draw_depth_order(jax.random.fold_in(splits[4], 71), 0),
    }


time_step = 0.4
weno_floor = 1e-6


def square(operand):
    return operand * operand


def weno_value(diff_one, diff_two, diff_three, diff_four, diff_five):
    candidate_one = diff_one / 3.0 - 7.0 * diff_two / 6.0 + 11.0 * diff_three / 6.0
    candidate_two = -diff_two / 6.0 + 5.0 * diff_three / 6.0 + diff_four / 3.0
    candidate_three = diff_three / 3.0 + 5.0 * diff_four / 6.0 - diff_five / 6.0
    smooth_one = 13.0 / 12.0 * square(diff_one - 2.0 * diff_two + diff_three) + 0.25 * square(diff_one - 4.0 * diff_two + 3.0 * diff_three)
    smooth_two = 13.0 / 12.0 * square(diff_two - 2.0 * diff_three + diff_four) + 0.25 * square(diff_two - diff_four)
    smooth_three = 13.0 / 12.0 * square(diff_three - 2.0 * diff_four + diff_five) + 0.25 * square(3.0 * diff_three - 4.0 * diff_four + diff_five)
    weight_one = 0.1 / square(weno_floor + smooth_one)
    weight_two = 0.6 / square(weno_floor + smooth_two)
    weight_three = 0.3 / square(weno_floor + smooth_three)
    return (weight_one * candidate_one + weight_two * candidate_two + weight_three * candidate_three) / (weight_one + weight_two + weight_three)


def shifted(level_field, axis_dim, offset):
    return jnp.roll(level_field, -offset, axis_dim)


def global_rate(level_field, velocity):
    summed = jnp.zeros(level_field.shape, jnp.float32)
    for axis_dim in range(3):
        jump_list = [shifted(level_field, axis_dim, offset) - shifted(level_field, axis_dim, offset - 1) for offset in range(-2, 4)]
        from_left = weno_value(jump_list[0], jump_list[1], jump_list[2], jump_list[3], jump_list[4])
        from_right = weno_value(jump_list[5], jump_list[4], jump_list[3], jump_list[2], jump_list[1])
        speed_axis = velocity[axis_dim].astype(jnp.float32)
        summed = summed + jnp.maximum(speed_axis, 0.0) * from_left + jnp.minimum(speed_axis, 0.0) * from_right
    return -summed


def shade(samples, alive, ascending):
    opacity = alive * (2.0 / CZ) / (1.0 + 4.0 * samples * samples)
    log_clear = jnp.log1p(-opacity)
    depth = jnp.arange(CZ)
    ahead = jnp.where(ascending, depth[:, None] < depth[None, :], depth[:, None] > depth[None, :]).astype(jnp.float32)
    flat_logs = log_clear.reshape(-1, CZ)
    before = jnp.dot(flat_logs, ahead, precision=lax.Precision.HIGHEST).reshape(log_clear.shape)
    weight = jnp.exp(before) * opacity
    bright = jnp.tanh(samples)
    red = jnp.sum(weight * (0.5 + 0.5 * bright), -1)
    green = jnp.sum(weight * (0.5 - 0.5 * bright), -1)
    blue = jnp.sum(weight / (1.0 + samples * samples), -1)
    clear = jnp.exp(jnp.sum(log_clear, -1))
    return jnp.stack([red, green, blue, clear])


def alternate(grid_pairs):
    row_list = [jnp.stack(pixel_pair, -1) for pixel_pair in grid_pairs]
    joined = jnp.stack(row_list, -3)
    joined_shape = joined.shape
    return joined.reshape(joined_shape[:-4] + (joined_shape[-4] * 2, joined_shape[-2] * 2))


def over(front_part, back_part):
    colour = front_part[:3] + front_part[3:] * back_part[:3]
    clear = front_part[3:] * back_part[3:]
    return jnp.concatenate([colour, clear], 0)


def reference(level_set, velocity, active_brick, depth_order):
    section_one = level_set + time_step * global_rate(level_set, velocity)
    section_two = 0.75 * level_set + 0.25 * (section_one + time_step * global_rate(section_one, velocity))
    advanced = level_set / 3.0 + (2.0 / 3.0) * (section_two + time_step * global_rate(section_two, velocity))
    active_cells = jnp.repeat(jnp.repeat(jnp.repeat(active_brick, CX, 0), CY, 1), CZ, 2)
    level_out = jnp.where(active_cells > 0, advanced, level_set)
    alive = active_cells.astype(jnp.float32).reshape(NX, NY, N_GZ, CZ)
    ascending = depth_order[0] < depth_order[N_GZ - 1]
    left_x = 0.75 * level_out + 0.25 * jnp.roll(level_out, 1, 0)
    right_x = 0.75 * level_out + 0.25 * jnp.roll(level_out, -1, 0)
    grid_pairs = []
    for along_x in (left_x, right_x):
        pair_list = []
        for neighbour in (jnp.roll(along_x, 1, 1), jnp.roll(along_x, -1, 1)):
            samples = (0.75 * along_x + 0.25 * neighbour).reshape(NX, NY, N_GZ, CZ)
            pair_list.append(jnp.moveaxis(shade(samples, alive, ascending), -1, 0))
        grid_pairs.append(pair_list)
    slab_images = alternate(grid_pairs)
    blended = jnp.concatenate([jnp.zeros((3, 2 * NX, 2 * NY), jnp.float32), jnp.ones((1, 2 * NX, 2 * NY), jnp.float32)], 0)
    for rank_value in range(N_GZ):
        chooser = (depth_order == rank_value).astype(jnp.float32)
        piece = jnp.einsum("s,schw->chw", chooser, slab_images, precision=lax.Precision.HIGHEST)
        blended = over(blended, piece)
    image = jnp.concatenate([blended[:3], 1.0 - blended[3:]], 0)
    return level_out, image
```

```python
import jax
import jax.numpy as jnp
from jax import lax
from jax.sharding import PartitionSpec as P

CZ = 128


time_step = 0.4
weno_floor = 1e-06


def extended(x, sides, width):
    for axis, dim in sides:
        size, length = (lax.axis_size(axis), x.shape[dim])
        up = [(i, (i + 1) % size) for i in range(size)]
        down = [(j, i) for i, j in up]
        last = lax.slice_in_dim(x, length - width, length, axis=dim)
        initial = lax.slice_in_dim(x, 0, width, axis=dim)
        before = lax.ppermute(last, axis, up)
        after = lax.ppermute(initial, axis, down)
        x = jnp.concatenate([before, x, after], axis=dim)
    return x


def faces(x, sides, width):
    padded = []
    for axis, dim in sides:
        size, length = (lax.axis_size(axis), x.shape[dim])
        up = [(i, (i + 1) % size) for i in range(size)]
        down = [(j, i) for i, j in up]
        last = lax.slice_in_dim(x, length - width, length, axis=dim)
        initial = lax.slice_in_dim(x, 0, width, axis=dim)
        before = lax.ppermute(last, axis, up)
        after = lax.ppermute(initial, axis, down)
        padded.append(jnp.concatenate([before, x, after], axis=dim))
    return padded


def rim_of(x):
    nx, ny = lax.axis_size("gx"), lax.axis_size("gy")
    lx, ly = x.shape[0], x.shape[1]
    pairs = {}
    for sx in (-1, 0, 1):
        for sy in (-1, 0, 1):
            if sx == 0 and sy == 0:
                continue
            pick_x = slice(0, 1) if sx == 1 else (slice(lx - 1, lx) if sx == -1 else slice(0, lx))
            pick_y = slice(0, 1) if sy == 1 else (slice(ly - 1, ly) if sy == -1 else slice(0, ly))
            perm = [
                (i * ny + j, ((i - sx) % nx) * ny + (j - sy) % ny)
                for i in range(nx)
                for j in range(ny)
            ]
            pairs[(sx, sy)] = lax.ppermute(x[pick_x, pick_y], ("gx", "gy"), perm)
    rows = []
    for sx in (-1, 0, 1):
        row = [pairs[(sx, -1)], x if sx == 0 else pairs[(sx, 0)], pairs[(sx, 1)]]
        rows.append(jnp.concatenate(row, axis=1))
    return jnp.concatenate(rows, axis=0)


def square(operand):
    return operand * operand


def weno_value(diff_one, diff_two, diff_three, diff_four, diff_five):
    candidate_one = diff_one / 3.0 - 7.0 * diff_two / 6.0 + 11.0 * diff_three / 6.0
    candidate_two = -diff_two / 6.0 + 5.0 * diff_three / 6.0 + diff_four / 3.0
    candidate_three = diff_three / 3.0 + 5.0 * diff_four / 6.0 - diff_five / 6.0
    smooth_one = 13.0 / 12.0 * square(diff_one - 2.0 * diff_two + diff_three) + 0.25 * square(
        diff_one - 4.0 * diff_two + 3.0 * diff_three
    )
    smooth_two = 13.0 / 12.0 * square(diff_two - 2.0 * diff_three + diff_four) + 0.25 * square(
        diff_two - diff_four
    )
    smooth_three = 13.0 / 12.0 * square(diff_three - 2.0 * diff_four + diff_five) + 0.25 * square(
        3.0 * diff_three - 4.0 * diff_four + diff_five
    )
    weight_one = 0.1 / square(weno_floor + smooth_one)
    weight_two = 0.6 / square(weno_floor + smooth_two)
    weight_three = 0.3 / square(weno_floor + smooth_three)
    return (
        weight_one * candidate_one + weight_two * candidate_two + weight_three * candidate_three
    ) / (weight_one + weight_two + weight_three)


def window(padded, axis_dim, offset):
    length = padded.shape[axis_dim] - 6
    return lax.slice_in_dim(padded, 3 + offset, 3 + offset + length, axis=axis_dim)


def local_rate(padded_list, velocity_window):
    summed = jnp.zeros(velocity_window.shape[1:], jnp.float32)
    for axis_dim in range(3):
        padded = padded_list[axis_dim]
        jump_list = [
            window(padded, axis_dim, offset) - window(padded, axis_dim, offset - 1)
            for offset in range(-2, 4)
        ]
        from_left = weno_value(jump_list[0], jump_list[1], jump_list[2], jump_list[3], jump_list[4])
        from_right = weno_value(
            jump_list[5], jump_list[4], jump_list[3], jump_list[2], jump_list[1]
        )
        speed_axis = velocity_window[axis_dim].astype(jnp.float32)
        summed = (
            summed
            + jnp.maximum(speed_axis, 0.0) * from_left
            + jnp.minimum(speed_axis, 0.0) * from_right
        )
    return -summed


def shade(samples, alive, ascending):
    opacity = alive * (2.0 / CZ) / (1.0 + 4.0 * samples * samples)
    log_clear = jnp.log1p(-opacity)
    depth = jnp.arange(CZ)
    ahead = jnp.where(
        ascending, depth[:, None] < depth[None, :], depth[:, None] > depth[None, :]
    ).astype(jnp.float32)
    flat_logs = log_clear.reshape(-1, CZ)
    before = jnp.dot(flat_logs, ahead, precision=lax.Precision.HIGHEST).reshape(log_clear.shape)
    weight = jnp.exp(before) * opacity
    bright = jnp.tanh(samples)
    red = jnp.sum(weight * (0.5 + 0.5 * bright), -1)
    green = jnp.sum(weight * (0.5 - 0.5 * bright), -1)
    blue = jnp.sum(weight / (1.0 + samples * samples), -1)
    clear = jnp.exp(jnp.sum(log_clear, -1))
    return jnp.stack([red, green, blue, clear])


def alternate(grid_pairs):
    row_list = [jnp.stack(pixel_pair, -1) for pixel_pair in grid_pairs]
    joined = jnp.stack(row_list, -3)
    joined_shape = joined.shape
    return joined.reshape(joined_shape[:-4] + (joined_shape[-4] * 2, joined_shape[-2] * 2))


def over(front_part, back_part):
    colour = front_part[:3] + front_part[3:] * back_part[:3]
    clear = front_part[3:] * back_part[3:]
    return jnp.concatenate([colour, clear], 0)


def shards(level_set, velocity, active_brick, depth_order):

    def section_rate(level_field):
        padded = faces(level_field, (("gx", 0), ("gy", 1), ("gz", 2)), 3)
        return local_rate(padded, velocity)

    section_one = level_set + time_step * section_rate(level_set)
    section_two = 0.75 * level_set + 0.25 * (section_one + time_step * section_rate(section_one))
    advanced = level_set / 3.0 + 2.0 / 3.0 * (section_two + time_step * section_rate(section_two))
    alive = active_brick[0, 0, 0] > 0
    level_out = jnp.where(alive, advanced, level_set)
    alive_float = alive.astype(jnp.float32)
    group = lax.axis_size("gz")
    ascending = depth_order[0] < depth_order[group - 1]
    rim = rim_of(level_out.astype(jnp.bfloat16)).astype(level_out.dtype)
    left_x = 0.75 * rim[1:-1] + 0.25 * rim[:-2]
    right_x = 0.75 * rim[1:-1] + 0.25 * rim[2:]
    grid_pairs = []
    for along_x in (left_x, right_x):
        pair_list = []
        for neighbour in (along_x[:, :-2], along_x[:, 2:]):
            samples = 0.75 * along_x[:, 1:-1] + 0.25 * neighbour
            pair_list.append(shade(samples, alive_float, ascending))
        grid_pairs.append(pair_list)
    slab_image = alternate(grid_pairs)
    rows_each = slab_image.shape[1] // group
    columns = slab_image.shape[2]
    pieces = slab_image.reshape(4, group, rows_each, columns)
    received = lax.all_to_all(pieces, "gz", split_axis=1, concat_axis=1, tiled=True)
    blended = jnp.concatenate(
        [
            jnp.zeros((3, rows_each, columns), jnp.float32),
            jnp.ones((1, rows_each, columns), jnp.float32),
        ],
        0,
    )
    for rank_value in range(group):
        chooser = (depth_order == rank_value).astype(jnp.float32)
        piece_now = jnp.einsum("s,csij->cij", chooser, received, precision=lax.Precision.HIGHEST)
        blended = over(blended, piece_now)
    image = jnp.concatenate([blended[:3], 1.0 - blended[3:]], 0)
    return (level_out, image)


def solution(mesh):
    placed = (P("gx", "gy", "gz"), P(None, "gx", "gy", "gz"), P("gx", "gy", "gz"), P())
    return jax.shard_map(
        shards,
        mesh=mesh,
        in_specs=placed,
        out_specs=(P("gx", "gy", "gz"), P(None, ("gx", "gz"), "gy")),
        check_vma=False,
    )
```

```python
import jax
import jax.numpy as jnp
from jax import lax
from jax.sharding import PartitionSpec as P

CZ = 128


time_step = 0.4
weno_floor = 1e-06
SPAN = 3


def exchange(fields, axis, widths, dim):
    size = lax.axis_size(axis)
    up = [(i, (i + 1) % size) for i in range(size)]
    down = [(j, i) for i, j in up]
    out = []
    for field, w in zip(fields, widths):
        d = dim + field.ndim - 3
        last = lax.slice_in_dim(field, field.shape[d] - w, field.shape[d], axis=d)
        first = lax.slice_in_dim(field, 0, w, axis=d)
        before = lax.ppermute(last, axis, up)
        after = lax.ppermute(first, axis, down)
        out.append(jnp.concatenate([before, field, after], axis=d))
    return out


def z_faces(x):
    size, length = (lax.axis_size("gz"), x.shape[2])
    up = [(i, (i + 1) % size) for i in range(size)]
    down = [(j, i) for i, j in up]
    before = lax.ppermute(x[:, :, length - SPAN :], "gz", up)
    after = lax.ppermute(x[:, :, :SPAN], "gz", down)
    return jnp.concatenate([before, x, after], axis=2)


def square(operand):
    return operand * operand


def weno_value(diff_one, diff_two, diff_three, diff_four, diff_five):
    candidate_one = diff_one / 3.0 - 7.0 * diff_two / 6.0 + 11.0 * diff_three / 6.0
    candidate_two = -diff_two / 6.0 + 5.0 * diff_three / 6.0 + diff_four / 3.0
    candidate_three = diff_three / 3.0 + 5.0 * diff_four / 6.0 - diff_five / 6.0
    smooth_one = 13.0 / 12.0 * square(diff_one - 2.0 * diff_two + diff_three) + 0.25 * square(
        diff_one - 4.0 * diff_two + 3.0 * diff_three
    )
    smooth_two = 13.0 / 12.0 * square(diff_two - 2.0 * diff_three + diff_four) + 0.25 * square(
        diff_two - diff_four
    )
    smooth_three = 13.0 / 12.0 * square(diff_three - 2.0 * diff_four + diff_five) + 0.25 * square(
        3.0 * diff_three - 4.0 * diff_four + diff_five
    )
    weight_one = 0.1 / square(weno_floor + smooth_one)
    weight_two = 0.6 / square(weno_floor + smooth_two)
    weight_three = 0.3 / square(weno_floor + smooth_three)
    return (
        weight_one * candidate_one + weight_two * candidate_two + weight_three * candidate_three
    ) / (weight_one + weight_two + weight_three)


def window(padded, axis_dim, offset):
    length = padded.shape[axis_dim] - 2 * SPAN
    return lax.slice_in_dim(padded, SPAN + offset, SPAN + offset + length, axis=axis_dim)


def local_rate(padded_list, speeds):
    summed = jnp.zeros(speeds.shape[1:], jnp.float32)
    for axis_dim in range(3):
        padded = padded_list[axis_dim]
        jump_list = [
            window(padded, axis_dim, offset) - window(padded, axis_dim, offset - 1)
            for offset in range(-2, 4)
        ]
        from_left = weno_value(jump_list[0], jump_list[1], jump_list[2], jump_list[3], jump_list[4])
        from_right = weno_value(
            jump_list[5], jump_list[4], jump_list[3], jump_list[2], jump_list[1]
        )
        speed_axis = speeds[axis_dim]
        summed = (
            summed
            + jnp.maximum(speed_axis, 0.0) * from_left
            + jnp.minimum(speed_axis, 0.0) * from_right
        )
    return -summed


def shade(samples, alive, ascending):
    opacity = alive * (2.0 / CZ) / (1.0 + 4.0 * samples * samples)
    log_clear = jnp.log1p(-opacity)
    depth = jnp.arange(CZ)
    ahead = jnp.where(
        ascending, depth[:, None] < depth[None, :], depth[:, None] > depth[None, :]
    ).astype(jnp.float32)
    flat_logs = log_clear.reshape(-1, CZ)
    before = jnp.dot(flat_logs, ahead, precision=lax.Precision.HIGHEST).reshape(log_clear.shape)
    weight = jnp.exp(before) * opacity
    bright = jnp.tanh(samples)
    red = jnp.sum(weight * (0.5 + 0.5 * bright), -1)
    green = jnp.sum(weight * (0.5 - 0.5 * bright), -1)
    blue = jnp.sum(weight / (1.0 + samples * samples), -1)
    clear = jnp.exp(jnp.sum(log_clear, -1))
    return jnp.stack([red, green, blue, clear])


def alternate(grid_pairs):
    row_list = [jnp.stack(pixel_pair, -1) for pixel_pair in grid_pairs]
    joined = jnp.stack(row_list, -3)
    joined_shape = joined.shape
    return joined.reshape(joined_shape[:-4] + (joined_shape[-4] * 2, joined_shape[-2] * 2))


def over(front_part, back_part):
    colour = front_part[:3] + front_part[3:] * back_part[:3]
    clear = front_part[3:] * back_part[3:]
    return jnp.concatenate([colour, clear], 0)


def stage_rate(field, speeds):
    inner = field[SPAN:-SPAN, SPAN:-SPAN]
    padded = [field[:, SPAN:-SPAN], field[SPAN:-SPAN, :], z_faces(inner)]
    return inner, local_rate(padded, speeds)


def shards(level_set, velocity, active_brick, depth_order):
    alive = active_brick[0, 0, 0] > 0
    alive_float = alive.astype(jnp.float32)
    flags = jnp.broadcast_to(alive_float, level_set.shape)
    stacked = jnp.stack([level_set] + [velocity[d].astype(jnp.float32) for d in range(3)] + [flags])
    halo = 3 * SPAN + 1
    stacked = exchange([stacked], "gx", [halo], 0)[0]
    stacked = exchange([stacked], "gy", [halo], 1)[0]
    level_ext = stacked[0]
    speed_ext = stacked[1:4, SPAN:-SPAN, SPAN:-SPAN]
    flag_ext = stacked[4, 3 * SPAN : -3 * SPAN, 3 * SPAN : -3 * SPAN]
    speed_two = speed_ext[:, SPAN:-SPAN, SPAN:-SPAN]
    speed_three = speed_two[:, SPAN:-SPAN, SPAN:-SPAN]

    inner, rate = stage_rate(level_ext, speed_ext)
    section_one = inner + time_step * rate
    inner, rate = stage_rate(section_one, speed_two)
    section_two = 0.75 * level_ext[2 * SPAN : -2 * SPAN, 2 * SPAN : -2 * SPAN] + 0.25 * (
        inner + time_step * rate
    )
    inner, rate = stage_rate(section_two, speed_three)
    level_ring = level_ext[3 * SPAN : -3 * SPAN, 3 * SPAN : -3 * SPAN]
    advanced = level_ring / 3.0 + 2.0 / 3.0 * (inner + time_step * rate)
    rim = jnp.where(flag_ext > 0, advanced, level_ring)
    level_out = rim[1:-1, 1:-1]

    group = lax.axis_size("gz")
    ascending = depth_order[0] < depth_order[group - 1]
    left_x = 0.75 * rim[1:-1] + 0.25 * rim[:-2]
    right_x = 0.75 * rim[1:-1] + 0.25 * rim[2:]
    grid_pairs = []
    for along_x in (left_x, right_x):
        pair_list = []
        for neighbour in (along_x[:, :-2], along_x[:, 2:]):
            samples = 0.75 * along_x[:, 1:-1] + 0.25 * neighbour
            pair_list.append(shade(samples, alive_float, ascending))
        grid_pairs.append(pair_list)
    slab_image = alternate(grid_pairs)
    rows_each = slab_image.shape[1] // group
    columns = slab_image.shape[2]
    pieces = slab_image.reshape(4, group, rows_each, columns)
    received = lax.all_to_all(pieces, "gz", split_axis=1, concat_axis=1, tiled=True)
    blended = jnp.concatenate(
        [
            jnp.zeros((3, rows_each, columns), jnp.float32),
            jnp.ones((1, rows_each, columns), jnp.float32),
        ],
        0,
    )
    for rank_value in range(group):
        chooser = (depth_order == rank_value).astype(jnp.float32)
        piece_now = jnp.einsum("s,csij->cij", chooser, received, precision=lax.Precision.HIGHEST)
        blended = over(blended, piece_now)
    image = jnp.concatenate([blended[:3], 1.0 - blended[3:]], 0)
    return (level_out, image)


def solution(mesh):
    placed = (P("gx", "gy", "gz"), P(None, "gx", "gy", "gz"), P("gx", "gy", "gz"), P())
    return jax.shard_map(
        shards,
        mesh=mesh,
        in_specs=placed,
        out_specs=(P("gx", "gy", "gz"), P(None, ("gx", "gz"), "gy")),
        check_vma=False,
    )
```

```python
import jax
import jax.numpy as jnp
from jax import lax
from jax.sharding import PartitionSpec as P

CZ = 128


time_step = 0.4
weno_floor = 1e-06
SPAN = 3


def exchange(fields, axis, widths, dim):
    size = lax.axis_size(axis)
    up = [(i, (i + 1) % size) for i in range(size)]
    down = [(j, i) for i, j in up]
    out = []
    for field, w in zip(fields, widths):
        d = dim + field.ndim - 3
        last = lax.slice_in_dim(field, field.shape[d] - w, field.shape[d], axis=d)
        first = lax.slice_in_dim(field, 0, w, axis=d)
        before = lax.ppermute(last, axis, up)
        after = lax.ppermute(first, axis, down)
        out.append(jnp.concatenate([before, field, after], axis=d))
    return out


def exchange_packed(fields, axis, widths):
    size = lax.axis_size(axis)
    up = [(i, (i + 1) % size) for i in range(size)]
    down = [(j, i) for i, j in up]
    dims = [field.ndim - 3 for field in fields]
    lasts = [
        lax.slice_in_dim(field, field.shape[d] - w, field.shape[d], axis=d)
        for field, w, d in zip(fields, widths, dims)
    ]
    firsts = [lax.slice_in_dim(field, 0, w, axis=d) for field, w, d in zip(fields, widths, dims)]

    def pack(parts):
        return jnp.concatenate([part.reshape(-1, part.shape[-1]) for part in parts], 0)

    def unpack(flat, like):
        out, at = [], 0
        for part in like:
            rows = part.size // part.shape[-1]
            out.append(flat[at : at + rows].reshape(part.shape))
            at += rows
        return out

    before = unpack(lax.ppermute(pack(lasts), axis, up), lasts)
    after = unpack(lax.ppermute(pack(firsts), axis, down), firsts)
    return [
        jnp.concatenate([b, field, a], axis=d)
        for b, field, a, d in zip(before, fields, after, dims)
    ]


def z_faces(x):
    size, length = (lax.axis_size("gz"), x.shape[2])
    up = [(i, (i + 1) % size) for i in range(size)]
    down = [(j, i) for i, j in up]
    before = lax.ppermute(x[:, :, length - SPAN :], "gz", up)
    after = lax.ppermute(x[:, :, :SPAN], "gz", down)
    return jnp.concatenate([before, x, after], axis=2)


def square(operand):
    return operand * operand


def weno_value(diff_one, diff_two, diff_three, diff_four, diff_five):
    candidate_one = diff_one / 3.0 - 7.0 * diff_two / 6.0 + 11.0 * diff_three / 6.0
    candidate_two = -diff_two / 6.0 + 5.0 * diff_three / 6.0 + diff_four / 3.0
    candidate_three = diff_three / 3.0 + 5.0 * diff_four / 6.0 - diff_five / 6.0
    smooth_one = 13.0 / 12.0 * square(diff_one - 2.0 * diff_two + diff_three) + 0.25 * square(
        diff_one - 4.0 * diff_two + 3.0 * diff_three
    )
    smooth_two = 13.0 / 12.0 * square(diff_two - 2.0 * diff_three + diff_four) + 0.25 * square(
        diff_two - diff_four
    )
    smooth_three = 13.0 / 12.0 * square(diff_three - 2.0 * diff_four + diff_five) + 0.25 * square(
        3.0 * diff_three - 4.0 * diff_four + diff_five
    )
    weight_one = 0.1 / square(weno_floor + smooth_one)
    weight_two = 0.6 / square(weno_floor + smooth_two)
    weight_three = 0.3 / square(weno_floor + smooth_three)
    return (
        weight_one * candidate_one + weight_two * candidate_two + weight_three * candidate_three
    ) / (weight_one + weight_two + weight_three)


def window(padded, axis_dim, offset):
    length = padded.shape[axis_dim] - 2 * SPAN
    return lax.slice_in_dim(padded, SPAN + offset, SPAN + offset + length, axis=axis_dim)


def local_rate(padded_list, speeds):
    summed = jnp.zeros(speeds.shape[1:], jnp.float32)
    for axis_dim in range(3):
        padded = padded_list[axis_dim]
        jump_list = [
            window(padded, axis_dim, offset) - window(padded, axis_dim, offset - 1)
            for offset in range(-2, 4)
        ]
        from_left = weno_value(jump_list[0], jump_list[1], jump_list[2], jump_list[3], jump_list[4])
        from_right = weno_value(
            jump_list[5], jump_list[4], jump_list[3], jump_list[2], jump_list[1]
        )
        speed_axis = speeds[axis_dim]
        summed = (
            summed
            + jnp.maximum(speed_axis, 0.0) * from_left
            + jnp.minimum(speed_axis, 0.0) * from_right
        )
    return -summed


def shade(samples, alive, ascending):
    opacity = alive * (2.0 / CZ) / (1.0 + 4.0 * samples * samples)
    log_clear = jnp.log1p(-opacity)
    depth = jnp.arange(CZ)
    ahead = jnp.where(
        ascending, depth[:, None] < depth[None, :], depth[:, None] > depth[None, :]
    ).astype(jnp.float32)
    flat_logs = log_clear.reshape(-1, CZ)
    before = jnp.dot(flat_logs, ahead, precision=lax.Precision.HIGHEST).reshape(log_clear.shape)
    weight = jnp.exp(before) * opacity
    bright = jnp.tanh(samples)
    red = jnp.sum(weight * (0.5 + 0.5 * bright), -1)
    green = jnp.sum(weight * (0.5 - 0.5 * bright), -1)
    blue = jnp.sum(weight / (1.0 + samples * samples), -1)
    clear = jnp.exp(jnp.sum(log_clear, -1))
    return jnp.stack([red, green, blue, clear])


def alternate(grid_pairs):
    row_list = [jnp.stack(pixel_pair, -1) for pixel_pair in grid_pairs]
    joined = jnp.stack(row_list, -3)
    joined_shape = joined.shape
    return joined.reshape(joined_shape[:-4] + (joined_shape[-4] * 2, joined_shape[-2] * 2))


def over(front_part, back_part):
    colour = front_part[:3] + front_part[3:] * back_part[:3]
    clear = front_part[3:] * back_part[3:]
    return jnp.concatenate([colour, clear], 0)


def stage_rate(field, speeds):
    inner = field[SPAN:-SPAN, SPAN:-SPAN]
    padded = [field[:, SPAN:-SPAN], field[SPAN:-SPAN, :], z_faces(inner)]
    return inner, local_rate(padded, speeds)


def shards(level_set, velocity, active_brick, depth_order):
    alive = active_brick[0, 0, 0] > 0
    alive_float = alive.astype(jnp.float32)
    flags = jnp.broadcast_to(alive_float, level_set.shape)
    speeds = velocity.astype(jnp.float32)
    halo, halo_speed = 3 * SPAN + 1, 2 * SPAN + 1
    level_x, speed_x, flag_x = exchange_packed(
        [level_set, speeds, flags], "gx", [halo, halo_speed, 1]
    )
    speed_x = jnp.pad(speed_x, ((0, 0), (halo - halo_speed,) * 2, (0, 0), (0, 0)))
    flag_x = jnp.pad(flag_x, ((halo - 1,) * 2, (0, 0), (0, 0)))
    stacked = jnp.concatenate([level_x[None], speed_x, flag_x[None]], 0)
    stacked = exchange([stacked], "gy", [halo], 1)[0]
    level_ext = stacked[0]
    speed_ext = stacked[1:4, SPAN:-SPAN, SPAN:-SPAN]
    flag_ext = stacked[4, 3 * SPAN : -3 * SPAN, 3 * SPAN : -3 * SPAN]
    speed_two = speed_ext[:, SPAN:-SPAN, SPAN:-SPAN]
    speed_three = speed_two[:, SPAN:-SPAN, SPAN:-SPAN]

    inner, rate = stage_rate(level_ext, speed_ext)
    section_one = inner + time_step * rate
    inner, rate = stage_rate(section_one, speed_two)
    section_two = 0.75 * level_ext[2 * SPAN : -2 * SPAN, 2 * SPAN : -2 * SPAN] + 0.25 * (
        inner + time_step * rate
    )
    inner, rate = stage_rate(section_two, speed_three)
    level_ring = level_ext[3 * SPAN : -3 * SPAN, 3 * SPAN : -3 * SPAN]
    advanced = level_ring / 3.0 + 2.0 / 3.0 * (inner + time_step * rate)
    rim = jnp.where(flag_ext > 0, advanced, level_ring)
    level_out = rim[1:-1, 1:-1]

    group = lax.axis_size("gz")
    ascending = depth_order[0] < depth_order[group - 1]
    left_x = 0.75 * rim[1:-1] + 0.25 * rim[:-2]
    right_x = 0.75 * rim[1:-1] + 0.25 * rim[2:]
    grid_pairs = []
    for along_x in (left_x, right_x):
        pair_list = []
        for neighbour in (along_x[:, :-2], along_x[:, 2:]):
            samples = 0.75 * along_x[:, 1:-1] + 0.25 * neighbour
            pair_list.append(shade(samples, alive_float, ascending))
        grid_pairs.append(pair_list)
    slab_image = alternate(grid_pairs)
    rows_each = slab_image.shape[1] // group
    columns = slab_image.shape[2]
    pieces = slab_image.reshape(4, group, rows_each, columns)
    received = lax.all_to_all(pieces, "gz", split_axis=1, concat_axis=1, tiled=True)
    blended = jnp.concatenate(
        [
            jnp.zeros((3, rows_each, columns), jnp.float32),
            jnp.ones((1, rows_each, columns), jnp.float32),
        ],
        0,
    )
    for rank_value in range(group):
        chooser = (depth_order == rank_value).astype(jnp.float32)
        piece_now = jnp.einsum("s,csij->cij", chooser, received, precision=lax.Precision.HIGHEST)
        blended = over(blended, piece_now)
    image = jnp.concatenate([blended[:3], 1.0 - blended[3:]], 0)
    return (level_out, image)


def solution(mesh):
    placed = (P("gx", "gy", "gz"), P(None, "gx", "gy", "gz"), P("gx", "gy", "gz"), P())
    return jax.shard_map(
        shards,
        mesh=mesh,
        in_specs=placed,
        out_specs=(P("gx", "gy", "gz"), P(None, ("gx", "gz"), "gy")),
        check_vma=False,
    )
```

```python
import jax
import jax.numpy as jnp
from jax import lax
from jax.sharding import PartitionSpec as P

CZ = 128


time_step = 0.4
weno_floor = 1e-06
SPAN = 3


def exchange(fields, axis, widths, dim):
    size = lax.axis_size(axis)
    up = [(i, (i + 1) % size) for i in range(size)]
    down = [(j, i) for i, j in up]
    out = []
    for field, w in zip(fields, widths):
        d = dim + field.ndim - 3
        last = lax.slice_in_dim(field, field.shape[d] - w, field.shape[d], axis=d)
        first = lax.slice_in_dim(field, 0, w, axis=d)
        before = lax.ppermute(last, axis, up)
        after = lax.ppermute(first, axis, down)
        out.append(jnp.concatenate([before, field, after], axis=d))
    return out


def exchange_packed(fields, axis, widths):
    size = lax.axis_size(axis)
    up = [(i, (i + 1) % size) for i in range(size)]
    down = [(j, i) for i, j in up]
    dims = [field.ndim - 3 for field in fields]
    lasts = [
        lax.slice_in_dim(field, field.shape[d] - w, field.shape[d], axis=d)
        for field, w, d in zip(fields, widths, dims)
    ]
    firsts = [lax.slice_in_dim(field, 0, w, axis=d) for field, w, d in zip(fields, widths, dims)]

    def pack(parts):
        return jnp.concatenate([part.reshape(-1, part.shape[-1]) for part in parts], 0)

    def unpack(flat, like):
        out, at = [], 0
        for part in like:
            rows = part.size // part.shape[-1]
            out.append(flat[at : at + rows].reshape(part.shape))
            at += rows
        return out

    before = unpack(lax.ppermute(pack(lasts), axis, up), lasts)
    after = unpack(lax.ppermute(pack(firsts), axis, down), firsts)
    return [
        jnp.concatenate([b, field, a], axis=d)
        for b, field, a, d in zip(before, fields, after, dims)
    ]


def z_faces(x):
    size, length = (lax.axis_size("gz"), x.shape[2])
    up = [(i, (i + 1) % size) for i in range(size)]
    down = [(j, i) for i, j in up]
    before = lax.ppermute(x[:, :, length - SPAN :], "gz", up)
    after = lax.ppermute(x[:, :, :SPAN], "gz", down)
    return jnp.concatenate([before, x, after], axis=2)


def square(operand):
    return operand * operand


def weno_value(diff_one, diff_two, diff_three, diff_four, diff_five):
    candidate_one = diff_one / 3.0 - 7.0 * diff_two / 6.0 + 11.0 * diff_three / 6.0
    candidate_two = -diff_two / 6.0 + 5.0 * diff_three / 6.0 + diff_four / 3.0
    candidate_three = diff_three / 3.0 + 5.0 * diff_four / 6.0 - diff_five / 6.0
    smooth_one = 13.0 / 12.0 * square(diff_one - 2.0 * diff_two + diff_three) + 0.25 * square(
        diff_one - 4.0 * diff_two + 3.0 * diff_three
    )
    smooth_two = 13.0 / 12.0 * square(diff_two - 2.0 * diff_three + diff_four) + 0.25 * square(
        diff_two - diff_four
    )
    smooth_three = 13.0 / 12.0 * square(diff_three - 2.0 * diff_four + diff_five) + 0.25 * square(
        3.0 * diff_three - 4.0 * diff_four + diff_five
    )
    guard_one = square(weno_floor + smooth_one)
    guard_two = square(weno_floor + smooth_two)
    guard_three = square(weno_floor + smooth_three)
    weight_one = 0.1 * (guard_two * guard_three)
    weight_two = 0.6 * (guard_one * guard_three)
    weight_three = 0.3 * (guard_one * guard_two)
    return (
        weight_one * candidate_one + weight_two * candidate_two + weight_three * candidate_three
    ) / (weight_one + weight_two + weight_three)


def window(padded, axis_dim, offset):
    length = padded.shape[axis_dim] - 2 * SPAN
    return lax.slice_in_dim(padded, SPAN + offset, SPAN + offset + length, axis=axis_dim)


def local_rate(padded_list, speeds):
    summed = jnp.zeros(speeds.shape[1:], jnp.float32)
    for axis_dim in range(3):
        padded = padded_list[axis_dim]
        jump_list = [
            window(padded, axis_dim, offset) - window(padded, axis_dim, offset - 1)
            for offset in range(-2, 4)
        ]
        from_left = weno_value(jump_list[0], jump_list[1], jump_list[2], jump_list[3], jump_list[4])
        from_right = weno_value(
            jump_list[5], jump_list[4], jump_list[3], jump_list[2], jump_list[1]
        )
        speed_axis = speeds[axis_dim]
        summed = (
            summed
            + jnp.maximum(speed_axis, 0.0) * from_left
            + jnp.minimum(speed_axis, 0.0) * from_right
        )
    return -summed


def shade(samples, alive, ascending):
    opacity = alive * (2.0 / CZ) / (1.0 + 4.0 * samples * samples)
    log_clear = jnp.log1p(-opacity)
    depth = jnp.arange(CZ)
    ahead = jnp.where(
        ascending, depth[:, None] < depth[None, :], depth[:, None] > depth[None, :]
    ).astype(jnp.float32)
    flat_logs = log_clear.reshape(-1, CZ)
    before = jnp.dot(flat_logs, ahead, precision=lax.Precision.HIGHEST).reshape(log_clear.shape)
    weight = jnp.exp(before) * opacity
    bright = jnp.tanh(samples)
    red = jnp.sum(weight * (0.5 + 0.5 * bright), -1)
    green = jnp.sum(weight * (0.5 - 0.5 * bright), -1)
    blue = jnp.sum(weight / (1.0 + samples * samples), -1)
    clear = jnp.exp(jnp.sum(log_clear, -1))
    return jnp.stack([red, green, blue, clear])


def alternate(grid_pairs):
    row_list = [jnp.stack(pixel_pair, -1) for pixel_pair in grid_pairs]
    joined = jnp.stack(row_list, -3)
    joined_shape = joined.shape
    return joined.reshape(joined_shape[:-4] + (joined_shape[-4] * 2, joined_shape[-2] * 2))


def over(front_part, back_part):
    colour = front_part[:3] + front_part[3:] * back_part[:3]
    clear = front_part[3:] * back_part[3:]
    return jnp.concatenate([colour, clear], 0)


def stage_rate(field, speeds):
    inner = field[SPAN:-SPAN, SPAN:-SPAN]
    padded = [field[:, SPAN:-SPAN], field[SPAN:-SPAN, :], z_faces(inner)]
    return inner, local_rate(padded, speeds)


def shards(level_set, velocity, active_brick, depth_order):
    alive = active_brick[0, 0, 0] > 0
    alive_float = alive.astype(jnp.float32)
    flags = jnp.broadcast_to(alive_float, level_set.shape)
    speeds = velocity.astype(jnp.float32)
    halo, halo_speed = 3 * SPAN + 1, 2 * SPAN + 1
    level_x, speed_x, flag_x = exchange_packed(
        [level_set, speeds, flags], "gx", [halo, halo_speed, 1]
    )
    speed_x = jnp.pad(speed_x, ((0, 0), (halo - halo_speed,) * 2, (0, 0), (0, 0)))
    flag_x = jnp.pad(flag_x, ((halo - 1,) * 2, (0, 0), (0, 0)))
    stacked = jnp.concatenate([level_x[None], speed_x, flag_x[None]], 0)
    stacked = exchange([stacked], "gy", [halo], 1)[0]
    level_ext = stacked[0]
    speed_ext = stacked[1:4, SPAN:-SPAN, SPAN:-SPAN]
    flag_ext = stacked[4, 3 * SPAN : -3 * SPAN, 3 * SPAN : -3 * SPAN]
    speed_two = speed_ext[:, SPAN:-SPAN, SPAN:-SPAN]
    speed_three = speed_two[:, SPAN:-SPAN, SPAN:-SPAN]

    inner, rate = stage_rate(level_ext, speed_ext)
    section_one = inner + time_step * rate
    inner, rate = stage_rate(section_one, speed_two)
    section_two = 0.75 * level_ext[2 * SPAN : -2 * SPAN, 2 * SPAN : -2 * SPAN] + 0.25 * (
        inner + time_step * rate
    )
    inner, rate = stage_rate(section_two, speed_three)
    level_ring = level_ext[3 * SPAN : -3 * SPAN, 3 * SPAN : -3 * SPAN]
    advanced = level_ring / 3.0 + 2.0 / 3.0 * (inner + time_step * rate)
    rim = jnp.where(flag_ext > 0, advanced, level_ring)
    level_out = rim[1:-1, 1:-1]

    group = lax.axis_size("gz")
    ascending = depth_order[0] < depth_order[group - 1]
    left_x = 0.75 * rim[1:-1] + 0.25 * rim[:-2]
    right_x = 0.75 * rim[1:-1] + 0.25 * rim[2:]
    grid_pairs = []
    for along_x in (left_x, right_x):
        pair_list = []
        for neighbour in (along_x[:, :-2], along_x[:, 2:]):
            samples = 0.75 * along_x[:, 1:-1] + 0.25 * neighbour
            pair_list.append(shade(samples, alive_float, ascending))
        grid_pairs.append(pair_list)
    slab_image = alternate(grid_pairs)
    rows_each = slab_image.shape[1] // group
    columns = slab_image.shape[2]
    pieces = slab_image.reshape(4, group, rows_each, columns)
    received = lax.all_to_all(pieces, "gz", split_axis=1, concat_axis=1, tiled=True)
    blended = jnp.concatenate(
        [
            jnp.zeros((3, rows_each, columns), jnp.float32),
            jnp.ones((1, rows_each, columns), jnp.float32),
        ],
        0,
    )
    for rank_value in range(group):
        chooser = (depth_order == rank_value).astype(jnp.float32)
        piece_now = jnp.einsum("s,csij->cij", chooser, received, precision=lax.Precision.HIGHEST)
        blended = over(blended, piece_now)
    image = jnp.concatenate([blended[:3], 1.0 - blended[3:]], 0)
    return (level_out, image)


def solution(mesh):
    placed = (P("gx", "gy", "gz"), P(None, "gx", "gy", "gz"), P("gx", "gy", "gz"), P())
    return jax.shard_map(
        shards,
        mesh=mesh,
        in_specs=placed,
        out_specs=(P("gx", "gy", "gz"), P(None, ("gx", "gz"), "gy")),
        check_vma=False,
    )
```

```python
import jax
import jax.numpy as jnp
from jax import lax
from jax.sharding import PartitionSpec as P

CZ = 128


time_step = 0.4
weno_floor = 1e-06
SPAN = 3


def exchange(fields, axis, widths, dim):
    size = lax.axis_size(axis)
    up = [(i, (i + 1) % size) for i in range(size)]
    down = [(j, i) for i, j in up]
    out = []
    for field, w in zip(fields, widths):
        d = dim + field.ndim - 3
        last = lax.slice_in_dim(field, field.shape[d] - w, field.shape[d], axis=d)
        first = lax.slice_in_dim(field, 0, w, axis=d)
        before = lax.ppermute(last, axis, up)
        after = lax.ppermute(first, axis, down)
        out.append(jnp.concatenate([before, field, after], axis=d))
    return out


def exchange_packed(fields, axis, widths):
    size = lax.axis_size(axis)
    up = [(i, (i + 1) % size) for i in range(size)]
    down = [(j, i) for i, j in up]
    dims = [field.ndim - 3 for field in fields]
    lasts = [
        lax.slice_in_dim(field, field.shape[d] - w, field.shape[d], axis=d)
        for field, w, d in zip(fields, widths, dims)
    ]
    firsts = [lax.slice_in_dim(field, 0, w, axis=d) for field, w, d in zip(fields, widths, dims)]

    def pack(parts):
        return jnp.concatenate([part.reshape(-1, part.shape[-1]) for part in parts], 0)

    def unpack(flat, like):
        out, at = [], 0
        for part in like:
            rows = part.size // part.shape[-1]
            out.append(flat[at : at + rows].reshape(part.shape))
            at += rows
        return out

    before = unpack(lax.ppermute(pack(lasts), axis, up), lasts)
    after = unpack(lax.ppermute(pack(firsts), axis, down), firsts)
    return [
        jnp.concatenate([b, field, a], axis=d)
        for b, field, a, d in zip(before, fields, after, dims)
    ]


def z_faces(x):
    size, length = (lax.axis_size("gz"), x.shape[2])
    up = [(i, (i + 1) % size) for i in range(size)]
    down = [(j, i) for i, j in up]
    before = lax.ppermute(x[:, :, length - SPAN :], "gz", up)
    after = lax.ppermute(x[:, :, :SPAN], "gz", down)
    return jnp.concatenate([before, x, after], axis=2)


def square(operand):
    return operand * operand


def weno_value(diff_one, diff_two, diff_three, diff_four, diff_five):
    candidate_one = diff_one / 3.0 - 7.0 * diff_two / 6.0 + 11.0 * diff_three / 6.0
    candidate_two = -diff_two / 6.0 + 5.0 * diff_three / 6.0 + diff_four / 3.0
    candidate_three = diff_three / 3.0 + 5.0 * diff_four / 6.0 - diff_five / 6.0
    smooth_one = 13.0 / 12.0 * square(diff_one - 2.0 * diff_two + diff_three) + 0.25 * square(
        diff_one - 4.0 * diff_two + 3.0 * diff_three
    )
    smooth_two = 13.0 / 12.0 * square(diff_two - 2.0 * diff_three + diff_four) + 0.25 * square(
        diff_two - diff_four
    )
    smooth_three = 13.0 / 12.0 * square(diff_three - 2.0 * diff_four + diff_five) + 0.25 * square(
        3.0 * diff_three - 4.0 * diff_four + diff_five
    )
    weight_one = 0.1 / square(weno_floor + smooth_one)
    weight_two = 0.6 / square(weno_floor + smooth_two)
    weight_three = 0.3 / square(weno_floor + smooth_three)
    return (
        weight_one * candidate_one + weight_two * candidate_two + weight_three * candidate_three
    ) / (weight_one + weight_two + weight_three)


def window(padded, axis_dim, offset):
    length = padded.shape[axis_dim] - 2 * SPAN
    return lax.slice_in_dim(padded, SPAN + offset, SPAN + offset + length, axis=axis_dim)


def local_rate(padded_list, speeds):
    summed = jnp.zeros(speeds.shape[1:], jnp.float32)
    for axis_dim in range(3):
        padded = padded_list[axis_dim]
        jump_list = [
            window(padded, axis_dim, offset) - window(padded, axis_dim, offset - 1)
            for offset in range(-2, 4)
        ]
        from_left = weno_value(jump_list[0], jump_list[1], jump_list[2], jump_list[3], jump_list[4])
        from_right = weno_value(
            jump_list[5], jump_list[4], jump_list[3], jump_list[2], jump_list[1]
        )
        speed_axis = speeds[axis_dim]
        summed = (
            summed
            + jnp.maximum(speed_axis, 0.0) * from_left
            + jnp.minimum(speed_axis, 0.0) * from_right
        )
    return -summed


def shade(samples, alive, ascending):
    opacity = alive * (2.0 / CZ) / (1.0 + 4.0 * samples * samples)
    log_clear = jnp.log1p(-opacity)
    depth = jnp.arange(CZ)
    ahead = jnp.where(
        ascending, depth[:, None] < depth[None, :], depth[:, None] > depth[None, :]
    ).astype(jnp.float32)
    flat_logs = log_clear.reshape(-1, CZ)
    before = jnp.dot(flat_logs, ahead, precision=lax.Precision.HIGHEST).reshape(log_clear.shape)
    weight = jnp.exp(before) * opacity
    bright = jnp.tanh(samples)
    red = jnp.sum(weight * (0.5 + 0.5 * bright), -1)
    green = jnp.sum(weight * (0.5 - 0.5 * bright), -1)
    blue = jnp.sum(weight / (1.0 + samples * samples), -1)
    clear = jnp.exp(jnp.sum(log_clear, -1))
    return jnp.stack([red, green, blue, clear])


def alternate(grid_pairs):
    row_list = [jnp.stack(pixel_pair, -1) for pixel_pair in grid_pairs]
    joined = jnp.stack(row_list, -3)
    joined_shape = joined.shape
    return joined.reshape(joined_shape[:-4] + (joined_shape[-4] * 2, joined_shape[-2] * 2))


def over(front_part, back_part):
    colour = front_part[:3] + front_part[3:] * back_part[:3]
    clear = front_part[3:] * back_part[3:]
    return jnp.concatenate([colour, clear], 0)


def x_faces(x, width):
    size, length = (lax.axis_size("gx"), x.shape[0])
    up = [(i, (i + 1) % size) for i in range(size)]
    down = [(j, i) for i, j in up]
    before = lax.ppermute(x[length - width :], "gx", up)
    after = lax.ppermute(x[:width], "gx", down)
    return jnp.concatenate([before, x, after], axis=0)


def stage_rate(field, speeds):
    inner = field[:, SPAN:-SPAN]
    padded = [x_faces(inner, SPAN), field, z_faces(inner)]
    return inner, local_rate(padded, speeds)


def shards(level_set, velocity, active_brick, depth_order):
    alive = active_brick[0, 0, 0] > 0
    alive_float = alive.astype(jnp.float32)
    flags = jnp.broadcast_to(alive_float, level_set.shape)
    stacked = jnp.stack([level_set] + [velocity[d].astype(jnp.float32) for d in range(3)] + [flags])
    halo = 3 * SPAN + 1
    stacked = exchange([stacked], "gy", [halo], 1)[0]
    level_ext = stacked[0]
    speed_one = stacked[1:4, :, SPAN:-SPAN]
    speed_two = speed_one[:, :, SPAN:-SPAN]
    speed_three = speed_two[:, :, SPAN:-SPAN]
    flag_ring = stacked[4, :, 3 * SPAN : -3 * SPAN]

    inner, rate = stage_rate(level_ext, speed_one)
    section_one = inner + time_step * rate
    inner, rate = stage_rate(section_one, speed_two)
    section_two = 0.75 * level_ext[:, 2 * SPAN : -2 * SPAN] + 0.25 * (inner + time_step * rate)
    inner, rate = stage_rate(section_two, speed_three)
    level_ring = level_ext[:, 3 * SPAN : -3 * SPAN]
    advanced = level_ring / 3.0 + 2.0 / 3.0 * (inner + time_step * rate)
    ringed = jnp.where(flag_ring > 0, advanced, level_ring)
    level_out = ringed[:, 1:-1]
    rim = x_faces(ringed, 1)

    group = lax.axis_size("gz")
    ascending = depth_order[0] < depth_order[group - 1]
    left_x = 0.75 * rim[1:-1] + 0.25 * rim[:-2]
    right_x = 0.75 * rim[1:-1] + 0.25 * rim[2:]
    grid_pairs = []
    for along_x in (left_x, right_x):
        pair_list = []
        for neighbour in (along_x[:, :-2], along_x[:, 2:]):
            samples = 0.75 * along_x[:, 1:-1] + 0.25 * neighbour
            pair_list.append(shade(samples, alive_float, ascending))
        grid_pairs.append(pair_list)
    slab_image = alternate(grid_pairs)
    rows_each = slab_image.shape[1] // group
    columns = slab_image.shape[2]
    pieces = slab_image.reshape(4, group, rows_each, columns)
    received = lax.all_to_all(pieces, "gz", split_axis=1, concat_axis=1, tiled=True)
    blended = jnp.concatenate(
        [
            jnp.zeros((3, rows_each, columns), jnp.float32),
            jnp.ones((1, rows_each, columns), jnp.float32),
        ],
        0,
    )
    for rank_value in range(group):
        chooser = (depth_order == rank_value).astype(jnp.float32)
        piece_now = jnp.einsum("s,csij->cij", chooser, received, precision=lax.Precision.HIGHEST)
        blended = over(blended, piece_now)
    image = jnp.concatenate([blended[:3], 1.0 - blended[3:]], 0)
    return (level_out, image)


def solution(mesh):
    placed = (P("gx", "gy", "gz"), P(None, "gx", "gy", "gz"), P("gx", "gy", "gz"), P())
    return jax.shard_map(
        shards,
        mesh=mesh,
        in_specs=placed,
        out_specs=(P("gx", "gy", "gz"), P(None, ("gx", "gz"), "gy")),
        check_vma=False,
    )
```

```python
import jax
import jax.numpy as jnp
from jax import lax
from jax.sharding import PartitionSpec as P

CZ = 128


time_step = 0.4
weno_floor = 1e-06
SPAN = 3


def exchange(fields, axis, widths, dim):
    size = lax.axis_size(axis)
    up = [(i, (i + 1) % size) for i in range(size)]
    down = [(j, i) for i, j in up]
    out = []
    for field, w in zip(fields, widths):
        d = dim + field.ndim - 3
        last = lax.slice_in_dim(field, field.shape[d] - w, field.shape[d], axis=d)
        first = lax.slice_in_dim(field, 0, w, axis=d)
        before = lax.ppermute(last, axis, up)
        after = lax.ppermute(first, axis, down)
        out.append(jnp.concatenate([before, field, after], axis=d))
    return out


def exchange_packed(fields, axis, widths):
    size = lax.axis_size(axis)
    up = [(i, (i + 1) % size) for i in range(size)]
    down = [(j, i) for i, j in up]
    dims = [field.ndim - 3 for field in fields]
    lasts = [
        lax.slice_in_dim(field, field.shape[d] - w, field.shape[d], axis=d)
        for field, w, d in zip(fields, widths, dims)
    ]
    firsts = [lax.slice_in_dim(field, 0, w, axis=d) for field, w, d in zip(fields, widths, dims)]

    def pack(parts):
        return jnp.concatenate([part.reshape(-1, part.shape[-1]) for part in parts], 0)

    def unpack(flat, like):
        out, at = [], 0
        for part in like:
            rows = part.size // part.shape[-1]
            out.append(flat[at : at + rows].reshape(part.shape))
            at += rows
        return out

    before = unpack(lax.ppermute(pack(lasts), axis, up), lasts)
    after = unpack(lax.ppermute(pack(firsts), axis, down), firsts)
    return [
        jnp.concatenate([b, field, a], axis=d)
        for b, field, a, d in zip(before, fields, after, dims)
    ]


def z_faces(x):
    size, length = (lax.axis_size("gz"), x.shape[2])
    up = [(i, (i + 1) % size) for i in range(size)]
    down = [(j, i) for i, j in up]
    before = lax.ppermute(x[:, :, length - SPAN :], "gz", up)
    after = lax.ppermute(x[:, :, :SPAN], "gz", down)
    return jnp.concatenate([before, x, after], axis=2)


def square(operand):
    return operand * operand


def weno_value(diff_one, diff_two, diff_three, diff_four, diff_five):
    candidate_one = diff_one / 3.0 - 7.0 * diff_two / 6.0 + 11.0 * diff_three / 6.0
    candidate_two = -diff_two / 6.0 + 5.0 * diff_three / 6.0 + diff_four / 3.0
    candidate_three = diff_three / 3.0 + 5.0 * diff_four / 6.0 - diff_five / 6.0
    smooth_one = 13.0 / 12.0 * square(diff_one - 2.0 * diff_two + diff_three) + 0.25 * square(
        diff_one - 4.0 * diff_two + 3.0 * diff_three
    )
    smooth_two = 13.0 / 12.0 * square(diff_two - 2.0 * diff_three + diff_four) + 0.25 * square(
        diff_two - diff_four
    )
    smooth_three = 13.0 / 12.0 * square(diff_three - 2.0 * diff_four + diff_five) + 0.25 * square(
        3.0 * diff_three - 4.0 * diff_four + diff_five
    )
    weight_one = 0.1 / square(weno_floor + smooth_one)
    weight_two = 0.6 / square(weno_floor + smooth_two)
    weight_three = 0.3 / square(weno_floor + smooth_three)
    return (
        weight_one * candidate_one + weight_two * candidate_two + weight_three * candidate_three
    ) / (weight_one + weight_two + weight_three)


def window(padded, axis_dim, offset):
    length = padded.shape[axis_dim] - 2 * SPAN
    return lax.slice_in_dim(padded, SPAN + offset, SPAN + offset + length, axis=axis_dim)


def local_rate(padded_list, speeds):
    summed = jnp.zeros(speeds.shape[1:], jnp.float32)
    for axis_dim in range(3):
        padded = padded_list[axis_dim]
        jump_list = [
            window(padded, axis_dim, offset) - window(padded, axis_dim, offset - 1)
            for offset in range(-2, 4)
        ]
        from_left = weno_value(jump_list[0], jump_list[1], jump_list[2], jump_list[3], jump_list[4])
        from_right = weno_value(
            jump_list[5], jump_list[4], jump_list[3], jump_list[2], jump_list[1]
        )
        speed_axis = speeds[axis_dim]
        summed = (
            summed
            + jnp.maximum(speed_axis, 0.0) * from_left
            + jnp.minimum(speed_axis, 0.0) * from_right
        )
    return -summed


def shade(samples, alive, ascending):
    opacity = alive * (2.0 / CZ) / (1.0 + 4.0 * samples * samples)
    log_clear = jnp.log1p(-opacity)
    depth = jnp.arange(CZ)
    ahead = jnp.where(
        ascending, depth[:, None] < depth[None, :], depth[:, None] > depth[None, :]
    ).astype(jnp.float32)
    flat_logs = log_clear.reshape(-1, CZ)
    before = jnp.dot(flat_logs, ahead, precision=lax.Precision.HIGHEST).reshape(log_clear.shape)
    weight = jnp.exp(before) * opacity
    bright = jnp.tanh(samples)
    red = jnp.sum(weight * (0.5 + 0.5 * bright), -1)
    green = jnp.sum(weight * (0.5 - 0.5 * bright), -1)
    blue = jnp.sum(weight / (1.0 + samples * samples), -1)
    clear = jnp.exp(jnp.sum(log_clear, -1))
    return jnp.stack([red, green, blue, clear])


def alternate(grid_pairs):
    row_list = [jnp.stack(pixel_pair, -1) for pixel_pair in grid_pairs]
    joined = jnp.stack(row_list, -3)
    joined_shape = joined.shape
    return joined.reshape(joined_shape[:-4] + (joined_shape[-4] * 2, joined_shape[-2] * 2))


def over(front_part, back_part):
    colour = front_part[:3] + front_part[3:] * back_part[:3]
    clear = front_part[3:] * back_part[3:]
    return jnp.concatenate([colour, clear], 0)


def x_faces(x, width):
    size, length = (lax.axis_size("gx"), x.shape[0])
    up = [(i, (i + 1) % size) for i in range(size)]
    down = [(j, i) for i, j in up]
    before = lax.ppermute(x[length - width :], "gx", up)
    after = lax.ppermute(x[:width], "gx", down)
    return jnp.concatenate([before, x, after], axis=0)


def stage_rate(field, speeds):
    inner = field[:, SPAN:-SPAN]
    padded = [x_faces(inner, SPAN), field, z_faces(inner)]
    return inner, local_rate(padded, speeds)


def shards(level_set, velocity, active_brick, depth_order):
    alive = active_brick[0, 0, 0] > 0
    alive_float = alive.astype(jnp.float32)
    flags = jnp.broadcast_to(alive_float, level_set.shape)
    stacked = jnp.stack([level_set] + [velocity[d].astype(jnp.float32) for d in range(3)] + [flags])
    halo = 3 * SPAN + 1
    stacked = exchange([stacked], "gy", [halo], 1)[0]
    level_ext = stacked[0]
    carried = stacked[1:5, :, SPAN:-SPAN]
    speed_one = carried[:3]
    speed_two = speed_one[:, :, SPAN:-SPAN]
    flag_ring = stacked[4, :, 3 * SPAN : -3 * SPAN]

    size = lax.axis_size("gx")
    up = [(i, (i + 1) % size) for i in range(size)]
    down = [(j, i) for i, j in up]
    inner = level_ext[:, SPAN:-SPAN]
    last = jnp.concatenate([inner[-SPAN:]] + [carried[c, -1:] for c in range(4)], 0)
    first = jnp.concatenate([inner[:SPAN]] + [carried[c, :1] for c in range(4)], 0)
    before = lax.ppermute(last, "gx", up)
    after = lax.ppermute(first, "gx", down)
    padded = [
        jnp.concatenate([before[:SPAN], inner, after[:SPAN]], 0),
        level_ext,
        z_faces(inner),
    ]
    section_one = inner + time_step * local_rate(padded, speed_one)
    inner, rate = stage_rate(section_one, speed_two)
    section_two = 0.75 * level_ext[:, 2 * SPAN : -2 * SPAN] + 0.25 * (inner + time_step * rate)

    ring = slice(2 * SPAN, -2 * SPAN)
    edge_before = before[SPAN - 1 :, ring]
    edge_after = jnp.concatenate([after[:1], after[SPAN:]], 0)[:, ring]
    wide = x_faces(section_two, SPAN + 1)
    inner = wide[SPAN:-SPAN, SPAN:-SPAN]
    padded = [wide[:, SPAN:-SPAN], wide[SPAN:-SPAN], z_faces(inner)]
    speed_three = jnp.concatenate(
        [edge_before[1:4][:, None], speed_two[:, :, SPAN:-SPAN], edge_after[1:4][:, None]], 1
    )
    rate = local_rate(padded, speed_three)
    level_ring = jnp.concatenate(
        [edge_before[:1], level_ext[:, 3 * SPAN : -3 * SPAN], edge_after[:1]], 0
    )
    flag_three = jnp.concatenate([edge_before[4:5], flag_ring, edge_after[4:5]], 0)
    advanced = level_ring / 3.0 + 2.0 / 3.0 * (inner + time_step * rate)
    rim = jnp.where(flag_three > 0, advanced, level_ring)
    level_out = rim[1:-1, 1:-1]

    group = lax.axis_size("gz")
    ascending = depth_order[0] < depth_order[group - 1]
    left_x = 0.75 * rim[1:-1] + 0.25 * rim[:-2]
    right_x = 0.75 * rim[1:-1] + 0.25 * rim[2:]
    grid_pairs = []
    for along_x in (left_x, right_x):
        pair_list = []
        for neighbour in (along_x[:, :-2], along_x[:, 2:]):
            samples = 0.75 * along_x[:, 1:-1] + 0.25 * neighbour
            pair_list.append(shade(samples, alive_float, ascending))
        grid_pairs.append(pair_list)
    slab_image = alternate(grid_pairs)
    rows_each = slab_image.shape[1] // group
    columns = slab_image.shape[2]
    pieces = slab_image.reshape(4, group, rows_each, columns)
    received = lax.all_to_all(pieces, "gz", split_axis=1, concat_axis=1, tiled=True)
    blended = jnp.concatenate(
        [
            jnp.zeros((3, rows_each, columns), jnp.float32),
            jnp.ones((1, rows_each, columns), jnp.float32),
        ],
        0,
    )
    for rank_value in range(group):
        chooser = (depth_order == rank_value).astype(jnp.float32)
        piece_now = jnp.einsum("s,csij->cij", chooser, received, precision=lax.Precision.HIGHEST)
        blended = over(blended, piece_now)
    image = jnp.concatenate([blended[:3], 1.0 - blended[3:]], 0)
    return (level_out, image)


def solution(mesh):
    placed = (P("gx", "gy", "gz"), P(None, "gx", "gy", "gz"), P("gx", "gy", "gz"), P())
    return jax.shard_map(
        shards,
        mesh=mesh,
        in_specs=placed,
        out_specs=(P("gx", "gy", "gz"), P(None, ("gx", "gz"), "gy")),
        check_vma=False,
    )
```

```python
import jax
import jax.numpy as jnp
from jax import lax
from jax.sharding import PartitionSpec as P

CZ = 128


time_step = 0.4
weno_floor = 1e-06
SPAN = 3


def exchange(fields, axis, widths, dim):
    size = lax.axis_size(axis)
    up = [(i, (i + 1) % size) for i in range(size)]
    down = [(j, i) for i, j in up]
    out = []
    for field, w in zip(fields, widths):
        d = dim + field.ndim - 3
        last = lax.slice_in_dim(field, field.shape[d] - w, field.shape[d], axis=d)
        first = lax.slice_in_dim(field, 0, w, axis=d)
        before = lax.ppermute(last, axis, up)
        after = lax.ppermute(first, axis, down)
        out.append(jnp.concatenate([before, field, after], axis=d))
    return out


def exchange_packed(fields, axis, widths):
    size = lax.axis_size(axis)
    up = [(i, (i + 1) % size) for i in range(size)]
    down = [(j, i) for i, j in up]
    dims = [field.ndim - 3 for field in fields]
    lasts = [
        lax.slice_in_dim(field, field.shape[d] - w, field.shape[d], axis=d)
        for field, w, d in zip(fields, widths, dims)
    ]
    firsts = [lax.slice_in_dim(field, 0, w, axis=d) for field, w, d in zip(fields, widths, dims)]

    def pack(parts):
        return jnp.concatenate([part.reshape(-1, part.shape[-1]) for part in parts], 0)

    def unpack(flat, like):
        out, at = [], 0
        for part in like:
            rows = part.size // part.shape[-1]
            out.append(flat[at : at + rows].reshape(part.shape))
            at += rows
        return out

    before = unpack(lax.ppermute(pack(lasts), axis, up), lasts)
    after = unpack(lax.ppermute(pack(firsts), axis, down), firsts)
    return [
        jnp.concatenate([b, field, a], axis=d)
        for b, field, a, d in zip(before, fields, after, dims)
    ]


def z_faces(x):
    size, length = (lax.axis_size("gz"), x.shape[2])
    up = [(i, (i + 1) % size) for i in range(size)]
    down = [(j, i) for i, j in up]
    before = lax.ppermute(x[:, :, length - SPAN :], "gz", up)
    after = lax.ppermute(x[:, :, :SPAN], "gz", down)
    return jnp.concatenate([before, x, after], axis=2)


def square(operand):
    return operand * operand


def weno_value(diff_one, diff_two, diff_three, diff_four, diff_five):
    candidate_one = diff_one / 3.0 - 7.0 * diff_two / 6.0 + 11.0 * diff_three / 6.0
    candidate_two = -diff_two / 6.0 + 5.0 * diff_three / 6.0 + diff_four / 3.0
    candidate_three = diff_three / 3.0 + 5.0 * diff_four / 6.0 - diff_five / 6.0
    smooth_one = 13.0 / 12.0 * square(diff_one - 2.0 * diff_two + diff_three) + 0.25 * square(
        diff_one - 4.0 * diff_two + 3.0 * diff_three
    )
    smooth_two = 13.0 / 12.0 * square(diff_two - 2.0 * diff_three + diff_four) + 0.25 * square(
        diff_two - diff_four
    )
    smooth_three = 13.0 / 12.0 * square(diff_three - 2.0 * diff_four + diff_five) + 0.25 * square(
        3.0 * diff_three - 4.0 * diff_four + diff_five
    )
    weight_one = 0.1 / square(weno_floor + smooth_one)
    weight_two = 0.6 / square(weno_floor + smooth_two)
    weight_three = 0.3 / square(weno_floor + smooth_three)
    return (
        weight_one * candidate_one + weight_two * candidate_two + weight_three * candidate_three
    ) / (weight_one + weight_two + weight_three)


def window(padded, axis_dim, offset):
    length = padded.shape[axis_dim] - 2 * SPAN
    return lax.slice_in_dim(padded, SPAN + offset, SPAN + offset + length, axis=axis_dim)


def local_rate(padded_list, speeds):
    summed = jnp.zeros(speeds.shape[1:], jnp.float32)
    for axis_dim in range(3):
        padded = padded_list[axis_dim]
        jump_list = [
            window(padded, axis_dim, offset) - window(padded, axis_dim, offset - 1)
            for offset in range(-2, 4)
        ]
        from_left = weno_value(jump_list[0], jump_list[1], jump_list[2], jump_list[3], jump_list[4])
        from_right = weno_value(
            jump_list[5], jump_list[4], jump_list[3], jump_list[2], jump_list[1]
        )
        speed_axis = speeds[axis_dim]
        summed = (
            summed
            + jnp.maximum(speed_axis, 0.0) * from_left
            + jnp.minimum(speed_axis, 0.0) * from_right
        )
    return -summed


def shade(samples, alive, ascending):
    opacity = alive * (2.0 / CZ) / (1.0 + 4.0 * samples * samples)
    log_clear = jnp.log1p(-opacity)
    depth = jnp.arange(CZ)
    ahead = jnp.where(
        ascending, depth[:, None] < depth[None, :], depth[:, None] > depth[None, :]
    ).astype(jnp.float32)
    flat_logs = log_clear.reshape(-1, CZ)
    before = jnp.dot(flat_logs, ahead, precision=lax.Precision.HIGHEST).reshape(log_clear.shape)
    weight = jnp.exp(before) * opacity
    bright = jnp.tanh(samples)
    red = jnp.sum(weight * (0.5 + 0.5 * bright), -1)
    green = jnp.sum(weight * (0.5 - 0.5 * bright), -1)
    blue = jnp.sum(weight / (1.0 + samples * samples), -1)
    clear = jnp.exp(jnp.sum(log_clear, -1))
    return jnp.stack([red, green, blue, clear])


def alternate(grid_pairs):
    row_list = [jnp.stack(pixel_pair, -1) for pixel_pair in grid_pairs]
    joined = jnp.stack(row_list, -3)
    joined_shape = joined.shape
    return joined.reshape(joined_shape[:-4] + (joined_shape[-4] * 2, joined_shape[-2] * 2))


def over(front_part, back_part):
    colour = front_part[:3] + front_part[3:] * back_part[:3]
    clear = front_part[3:] * back_part[3:]
    return jnp.concatenate([colour, clear], 0)


def x_faces(x, width):
    size, length = (lax.axis_size("gx"), x.shape[0])
    up = [(i, (i + 1) % size) for i in range(size)]
    down = [(j, i) for i, j in up]
    before = lax.ppermute(x[length - width :], "gx", up)
    after = lax.ppermute(x[:width], "gx", down)
    return jnp.concatenate([before, x, after], axis=0)


def stage_rate(field, speeds):
    inner = field[:, SPAN:-SPAN]
    padded = [x_faces(inner, SPAN), field, z_faces(inner)]
    return inner, local_rate(padded, speeds)


def shards(level_set, velocity, active_brick, depth_order):
    alive = active_brick[0, 0, 0] > 0
    alive_float = alive.astype(jnp.float32)
    flags = jnp.broadcast_to(alive_float, level_set.shape)
    fields = [level_set] + [velocity[d].astype(jnp.float32) for d in range(3)] + [flags]
    halo, halo_speed = 3 * SPAN + 1, 2 * SPAN + 1
    size, length = (lax.axis_size("gy"), level_set.shape[1])
    up = [(i, (i + 1) % size) for i in range(size)]
    down = [(j, i) for i, j in up]
    before = lax.ppermute(jnp.stack([f[:, length - halo :] for f in fields]), "gy", up)
    after = lax.ppermute(jnp.stack([f[:, :halo] for f in fields]), "gy", down)

    def grown(c, w):
        return jnp.concatenate([before[c, :, halo - w :], fields[c], after[c, :, :w]], axis=1)

    level_ext = grown(0, halo)
    speed_one = jnp.stack([grown(c, halo_speed) for c in range(1, 4)])
    speed_two = speed_one[:, :, SPAN:-SPAN]
    speed_three = speed_two[:, :, SPAN:-SPAN]
    flag_ring = grown(4, 1)

    inner, rate = stage_rate(level_ext, speed_one)
    section_one = inner + time_step * rate
    inner, rate = stage_rate(section_one, speed_two)
    section_two = 0.75 * level_ext[:, 2 * SPAN : -2 * SPAN] + 0.25 * (inner + time_step * rate)
    inner, rate = stage_rate(section_two, speed_three)
    level_ring = level_ext[:, 3 * SPAN : -3 * SPAN]
    advanced = level_ring / 3.0 + 2.0 / 3.0 * (inner + time_step * rate)
    ringed = jnp.where(flag_ring > 0, advanced, level_ring)
    level_out = ringed[:, 1:-1]
    rim = x_faces(ringed, 1)

    group = lax.axis_size("gz")
    ascending = depth_order[0] < depth_order[group - 1]
    left_x = 0.75 * rim[1:-1] + 0.25 * rim[:-2]
    right_x = 0.75 * rim[1:-1] + 0.25 * rim[2:]
    grid_pairs = []
    for along_x in (left_x, right_x):
        pair_list = []
        for neighbour in (along_x[:, :-2], along_x[:, 2:]):
            samples = 0.75 * along_x[:, 1:-1] + 0.25 * neighbour
            pair_list.append(shade(samples, alive_float, ascending))
        grid_pairs.append(pair_list)
    slab_image = alternate(grid_pairs)
    rows_each = slab_image.shape[1] // group
    columns = slab_image.shape[2]
    pieces = slab_image.reshape(4, group, rows_each, columns)
    received = lax.all_to_all(pieces, "gz", split_axis=1, concat_axis=1, tiled=True)
    blended = jnp.concatenate(
        [
            jnp.zeros((3, rows_each, columns), jnp.float32),
            jnp.ones((1, rows_each, columns), jnp.float32),
        ],
        0,
    )
    for rank_value in range(group):
        chooser = (depth_order == rank_value).astype(jnp.float32)
        piece_now = jnp.einsum("s,csij->cij", chooser, received, precision=lax.Precision.HIGHEST)
        blended = over(blended, piece_now)
    image = jnp.concatenate([blended[:3], 1.0 - blended[3:]], 0)
    return (level_out, image)


def solution(mesh):
    placed = (P("gx", "gy", "gz"), P(None, "gx", "gy", "gz"), P("gx", "gy", "gz"), P())
    return jax.shard_map(
        shards,
        mesh=mesh,
        in_specs=placed,
        out_specs=(P("gx", "gy", "gz"), P(None, ("gx", "gz"), "gy")),
        check_vma=False,
    )
```

```python
import jax
import jax.numpy as jnp
from jax import lax
from jax.sharding import PartitionSpec as P

CZ = 128


time_step = 0.4
weno_floor = 1e-06
SPAN = 3


def exchange(fields, axis, widths, dim):
    size = lax.axis_size(axis)
    up = [(i, (i + 1) % size) for i in range(size)]
    down = [(j, i) for i, j in up]
    out = []
    for field, w in zip(fields, widths):
        d = dim + field.ndim - 3
        last = lax.slice_in_dim(field, field.shape[d] - w, field.shape[d], axis=d)
        first = lax.slice_in_dim(field, 0, w, axis=d)
        before = lax.ppermute(last, axis, up)
        after = lax.ppermute(first, axis, down)
        out.append(jnp.concatenate([before, field, after], axis=d))
    return out


def exchange_packed(fields, axis, widths):
    size = lax.axis_size(axis)
    up = [(i, (i + 1) % size) for i in range(size)]
    down = [(j, i) for i, j in up]
    dims = [field.ndim - 3 for field in fields]
    lasts = [
        lax.slice_in_dim(field, field.shape[d] - w, field.shape[d], axis=d)
        for field, w, d in zip(fields, widths, dims)
    ]
    firsts = [lax.slice_in_dim(field, 0, w, axis=d) for field, w, d in zip(fields, widths, dims)]

    def pack(parts):
        return jnp.concatenate([part.reshape(-1, part.shape[-1]) for part in parts], 0)

    def unpack(flat, like):
        out, at = [], 0
        for part in like:
            rows = part.size // part.shape[-1]
            out.append(flat[at : at + rows].reshape(part.shape))
            at += rows
        return out

    before = unpack(lax.ppermute(pack(lasts), axis, up), lasts)
    after = unpack(lax.ppermute(pack(firsts), axis, down), firsts)
    return [
        jnp.concatenate([b, field, a], axis=d)
        for b, field, a, d in zip(before, fields, after, dims)
    ]


def z_faces(x):
    size, length = (lax.axis_size("gz"), x.shape[2])
    up = [(i, (i + 1) % size) for i in range(size)]
    down = [(j, i) for i, j in up]
    before = lax.ppermute(x[:, :, length - SPAN :], "gz", up)
    after = lax.ppermute(x[:, :, :SPAN], "gz", down)
    return jnp.concatenate([before, x, after], axis=2)


def square(operand):
    return operand * operand


def weno_value(diff_one, diff_two, diff_three, diff_four, diff_five):
    candidate_one = diff_one / 3.0 - 7.0 * diff_two / 6.0 + 11.0 * diff_three / 6.0
    candidate_two = -diff_two / 6.0 + 5.0 * diff_three / 6.0 + diff_four / 3.0
    candidate_three = diff_three / 3.0 + 5.0 * diff_four / 6.0 - diff_five / 6.0
    smooth_one = 13.0 / 12.0 * square(diff_one - 2.0 * diff_two + diff_three) + 0.25 * square(
        diff_one - 4.0 * diff_two + 3.0 * diff_three
    )
    smooth_two = 13.0 / 12.0 * square(diff_two - 2.0 * diff_three + diff_four) + 0.25 * square(
        diff_two - diff_four
    )
    smooth_three = 13.0 / 12.0 * square(diff_three - 2.0 * diff_four + diff_five) + 0.25 * square(
        3.0 * diff_three - 4.0 * diff_four + diff_five
    )
    weight_one = 0.1 / square(weno_floor + smooth_one)
    weight_two = 0.6 / square(weno_floor + smooth_two)
    weight_three = 0.3 / square(weno_floor + smooth_three)
    return (
        weight_one * candidate_one + weight_two * candidate_two + weight_three * candidate_three
    ) / (weight_one + weight_two + weight_three)


def window(padded, axis_dim, offset):
    length = padded.shape[axis_dim] - 2 * SPAN
    return lax.slice_in_dim(padded, SPAN + offset, SPAN + offset + length, axis=axis_dim)


def local_rate(padded_list, speeds):
    summed = jnp.zeros(speeds.shape[1:], jnp.float32)
    for axis_dim in range(3):
        padded = padded_list[axis_dim]
        jump_list = [
            window(padded, axis_dim, offset) - window(padded, axis_dim, offset - 1)
            for offset in range(-2, 4)
        ]
        from_left = weno_value(jump_list[0], jump_list[1], jump_list[2], jump_list[3], jump_list[4])
        from_right = weno_value(
            jump_list[5], jump_list[4], jump_list[3], jump_list[2], jump_list[1]
        )
        speed_axis = speeds[axis_dim]
        summed = (
            summed
            + jnp.maximum(speed_axis, 0.0) * from_left
            + jnp.minimum(speed_axis, 0.0) * from_right
        )
    return -summed


def shade(samples, alive, ascending):
    opacity = alive * (2.0 / CZ) / (1.0 + 4.0 * samples * samples)
    log_clear = jnp.log1p(-opacity)
    depth = jnp.arange(CZ)
    ahead = jnp.where(
        ascending, depth[:, None] < depth[None, :], depth[:, None] > depth[None, :]
    ).astype(jnp.float32)
    flat_logs = log_clear.reshape(-1, CZ)
    before = jnp.dot(flat_logs, ahead, precision=lax.Precision.HIGHEST).reshape(log_clear.shape)
    weight = jnp.exp(before) * opacity
    bright = jnp.tanh(samples)
    red = jnp.sum(weight * (0.5 + 0.5 * bright), -1)
    green = jnp.sum(weight * (0.5 - 0.5 * bright), -1)
    blue = jnp.sum(weight / (1.0 + samples * samples), -1)
    clear = jnp.exp(jnp.sum(log_clear, -1))
    return jnp.stack([red, green, blue, clear])


def alternate(grid_pairs):
    row_list = [jnp.stack(pixel_pair, -1) for pixel_pair in grid_pairs]
    joined = jnp.stack(row_list, -3)
    joined_shape = joined.shape
    return joined.reshape(joined_shape[:-4] + (joined_shape[-4] * 2, joined_shape[-2] * 2))


def over(front_part, back_part):
    colour = front_part[:3] + front_part[3:] * back_part[:3]
    clear = front_part[3:] * back_part[3:]
    return jnp.concatenate([colour, clear], 0)


def x_faces(x, width):
    size, length = (lax.axis_size("gx"), x.shape[0])
    up = [(i, (i + 1) % size) for i in range(size)]
    down = [(j, i) for i, j in up]
    before = lax.ppermute(x[length - width :], "gx", up)
    after = lax.ppermute(x[:width], "gx", down)
    return jnp.concatenate([before, x, after], axis=0)


def stage_rate(field, speeds):
    inner = field[:, SPAN:-SPAN]
    padded = [x_faces(inner, SPAN), field, z_faces(inner)]
    return inner, local_rate(padded, speeds)


def shards(level_set, velocity, active_brick, depth_order):
    alive = active_brick[0, 0, 0] > 0
    alive_float = alive.astype(jnp.float32)
    stacked = jnp.stack([level_set] + [velocity[d].astype(jnp.float32) for d in range(3)])
    halo = 3 * SPAN + 1
    size, length = (lax.axis_size("gy"), stacked.shape[2])
    up = [(i, (i + 1) % size) for i in range(size)]
    down = [(j, i) for i, j in up]
    last = stacked[:, :, length - halo :]
    first = stacked[:, :, :halo]
    last = last.at[1, :, 0].set(alive_float)
    first = first.at[1, :, halo - 1].set(alive_float)
    before = lax.ppermute(last, "gy", up)
    after = lax.ppermute(first, "gy", down)
    stacked = jnp.concatenate([before, stacked, after], axis=2)
    level_ext = stacked[0]
    speed_one = stacked[1:4, :, SPAN:-SPAN]
    speed_two = speed_one[:, :, SPAN:-SPAN]
    speed_three = speed_two[:, :, SPAN:-SPAN]
    ring_width = length + 2
    place = lax.broadcasted_iota(jnp.int32, (1, ring_width, 1), 1)
    flag_ring = jnp.where(
        place == 0,
        before[1, 0, 0, 0],
        jnp.where(place == ring_width - 1, after[1, 0, halo - 1, 0], alive_float),
    )

    inner, rate = stage_rate(level_ext, speed_one)
    section_one = inner + time_step * rate
    inner, rate = stage_rate(section_one, speed_two)
    section_two = 0.75 * level_ext[:, 2 * SPAN : -2 * SPAN] + 0.25 * (inner + time_step * rate)
    inner, rate = stage_rate(section_two, speed_three)
    level_ring = level_ext[:, 3 * SPAN : -3 * SPAN]
    advanced = level_ring / 3.0 + 2.0 / 3.0 * (inner + time_step * rate)
    ringed = jnp.where(flag_ring > 0, advanced, level_ring)
    level_out = ringed[:, 1:-1]
    rim = x_faces(ringed, 1)

    group = lax.axis_size("gz")
    ascending = depth_order[0] < depth_order[group - 1]
    left_x = 0.75 * rim[1:-1] + 0.25 * rim[:-2]
    right_x = 0.75 * rim[1:-1] + 0.25 * rim[2:]
    grid_pairs = []
    for along_x in (left_x, right_x):
        pair_list = []
        for neighbour in (along_x[:, :-2], along_x[:, 2:]):
            samples = 0.75 * along_x[:, 1:-1] + 0.25 * neighbour
            pair_list.append(shade(samples, alive_float, ascending))
        grid_pairs.append(pair_list)
    slab_image = alternate(grid_pairs)
    rows_each = slab_image.shape[1] // group
    columns = slab_image.shape[2]
    pieces = slab_image.reshape(4, group, rows_each, columns)
    received = lax.all_to_all(pieces, "gz", split_axis=1, concat_axis=1, tiled=True)
    blended = jnp.concatenate(
        [
            jnp.zeros((3, rows_each, columns), jnp.float32),
            jnp.ones((1, rows_each, columns), jnp.float32),
        ],
        0,
    )
    for rank_value in range(group):
        chooser = (depth_order == rank_value).astype(jnp.float32)
        piece_now = jnp.einsum("s,csij->cij", chooser, received, precision=lax.Precision.HIGHEST)
        blended = over(blended, piece_now)
    image = jnp.concatenate([blended[:3], 1.0 - blended[3:]], 0)
    return (level_out, image)


def solution(mesh):
    placed = (P("gx", "gy", "gz"), P(None, "gx", "gy", "gz"), P("gx", "gy", "gz"), P())
    return jax.shard_map(
        shards,
        mesh=mesh,
        in_specs=placed,
        out_specs=(P("gx", "gy", "gz"), P(None, ("gx", "gz"), "gy")),
        check_vma=False,
    )
```

```python
import jax
import jax.numpy as jnp
from jax import lax
from jax.sharding import PartitionSpec as P

CZ = 128


time_step = 0.4
weno_floor = 1e-06
SPAN = 3


def exchange(fields, axis, widths, dim):
    size = lax.axis_size(axis)
    up = [(i, (i + 1) % size) for i in range(size)]
    down = [(j, i) for i, j in up]
    out = []
    for field, w in zip(fields, widths):
        d = dim + field.ndim - 3
        last = lax.slice_in_dim(field, field.shape[d] - w, field.shape[d], axis=d)
        first = lax.slice_in_dim(field, 0, w, axis=d)
        before = lax.ppermute(last, axis, up)
        after = lax.ppermute(first, axis, down)
        out.append(jnp.concatenate([before, field, after], axis=d))
    return out


def exchange_packed(fields, axis, widths):
    size = lax.axis_size(axis)
    up = [(i, (i + 1) % size) for i in range(size)]
    down = [(j, i) for i, j in up]
    dims = [field.ndim - 3 for field in fields]
    lasts = [
        lax.slice_in_dim(field, field.shape[d] - w, field.shape[d], axis=d)
        for field, w, d in zip(fields, widths, dims)
    ]
    firsts = [lax.slice_in_dim(field, 0, w, axis=d) for field, w, d in zip(fields, widths, dims)]

    def pack(parts):
        return jnp.concatenate([part.reshape(-1, part.shape[-1]) for part in parts], 0)

    def unpack(flat, like):
        out, at = [], 0
        for part in like:
            rows = part.size // part.shape[-1]
            out.append(flat[at : at + rows].reshape(part.shape))
            at += rows
        return out

    before = unpack(lax.ppermute(pack(lasts), axis, up), lasts)
    after = unpack(lax.ppermute(pack(firsts), axis, down), firsts)
    return [
        jnp.concatenate([b, field, a], axis=d)
        for b, field, a, d in zip(before, fields, after, dims)
    ]


def z_faces(x):
    size, length = (lax.axis_size("gz"), x.shape[2])
    up = [(i, (i + 1) % size) for i in range(size)]
    down = [(j, i) for i, j in up]
    before = lax.ppermute(x[:, :, length - SPAN :], "gz", up)
    after = lax.ppermute(x[:, :, :SPAN], "gz", down)
    return jnp.concatenate([before, x, after], axis=2)


def square(operand):
    return operand * operand


def weno_value(diff_one, diff_two, diff_three, diff_four, diff_five):
    candidate_one = diff_one / 3.0 - 7.0 * diff_two / 6.0 + 11.0 * diff_three / 6.0
    candidate_two = -diff_two / 6.0 + 5.0 * diff_three / 6.0 + diff_four / 3.0
    candidate_three = diff_three / 3.0 + 5.0 * diff_four / 6.0 - diff_five / 6.0
    smooth_one = 13.0 / 12.0 * square(diff_one - 2.0 * diff_two + diff_three) + 0.25 * square(
        diff_one - 4.0 * diff_two + 3.0 * diff_three
    )
    smooth_two = 13.0 / 12.0 * square(diff_two - 2.0 * diff_three + diff_four) + 0.25 * square(
        diff_two - diff_four
    )
    smooth_three = 13.0 / 12.0 * square(diff_three - 2.0 * diff_four + diff_five) + 0.25 * square(
        3.0 * diff_three - 4.0 * diff_four + diff_five
    )
    weight_one = 0.1 / square(weno_floor + smooth_one)
    weight_two = 0.6 / square(weno_floor + smooth_two)
    weight_three = 0.3 / square(weno_floor + smooth_three)
    return (
        weight_one * candidate_one + weight_two * candidate_two + weight_three * candidate_three
    ) / (weight_one + weight_two + weight_three)


def window(padded, axis_dim, offset):
    length = padded.shape[axis_dim] - 2 * SPAN
    return lax.slice_in_dim(padded, SPAN + offset, SPAN + offset + length, axis=axis_dim)


def local_rate(padded_list, speeds):
    summed = jnp.zeros(speeds.shape[1:], jnp.float32)
    for axis_dim in range(3):
        padded = padded_list[axis_dim]
        jump_list = [
            window(padded, axis_dim, offset) - window(padded, axis_dim, offset - 1)
            for offset in range(-2, 4)
        ]
        from_left = weno_value(jump_list[0], jump_list[1], jump_list[2], jump_list[3], jump_list[4])
        from_right = weno_value(
            jump_list[5], jump_list[4], jump_list[3], jump_list[2], jump_list[1]
        )
        speed_axis = speeds[axis_dim]
        summed = (
            summed
            + jnp.maximum(speed_axis, 0.0) * from_left
            + jnp.minimum(speed_axis, 0.0) * from_right
        )
    return -summed


def shade(samples, alive, ascending):
    opacity = alive * (2.0 / CZ) / (1.0 + 4.0 * samples * samples)
    log_clear = jnp.log1p(-opacity)
    depth = jnp.arange(CZ)
    ahead = jnp.where(
        ascending, depth[:, None] < depth[None, :], depth[:, None] > depth[None, :]
    ).astype(jnp.float32)
    flat_logs = log_clear.reshape(-1, CZ)
    before = jnp.dot(flat_logs, ahead, precision=lax.Precision.HIGH).reshape(log_clear.shape)
    weight = jnp.exp(before) * opacity
    bright = jnp.tanh(samples)
    red = jnp.sum(weight * (0.5 + 0.5 * bright), -1)
    green = jnp.sum(weight * (0.5 - 0.5 * bright), -1)
    blue = jnp.sum(weight / (1.0 + samples * samples), -1)
    clear = jnp.exp(jnp.sum(log_clear, -1))
    return jnp.stack([red, green, blue, clear])


def alternate(grid_pairs):
    row_list = [jnp.stack(pixel_pair, -1) for pixel_pair in grid_pairs]
    joined = jnp.stack(row_list, -3)
    joined_shape = joined.shape
    return joined.reshape(joined_shape[:-4] + (joined_shape[-4] * 2, joined_shape[-2] * 2))


def over(front_part, back_part):
    colour = front_part[:3] + front_part[3:] * back_part[:3]
    clear = front_part[3:] * back_part[3:]
    return jnp.concatenate([colour, clear], 0)


def x_faces(x, width):
    size, length = (lax.axis_size("gx"), x.shape[0])
    up = [(i, (i + 1) % size) for i in range(size)]
    down = [(j, i) for i, j in up]
    before = lax.ppermute(x[length - width :], "gx", up)
    after = lax.ppermute(x[:width], "gx", down)
    return jnp.concatenate([before, x, after], axis=0)


def stage_rate(field, speeds):
    inner = field[:, SPAN:-SPAN]
    padded = [x_faces(inner, SPAN), field, z_faces(inner)]
    return inner, local_rate(padded, speeds)


def shards(level_set, velocity, active_brick, depth_order):
    alive = active_brick[0, 0, 0] > 0
    alive_float = alive.astype(jnp.float32)
    stacked = jnp.stack([level_set] + [velocity[d].astype(jnp.float32) for d in range(3)])
    halo = 3 * SPAN + 1
    size, length = (lax.axis_size("gy"), stacked.shape[2])
    up = [(i, (i + 1) % size) for i in range(size)]
    down = [(j, i) for i, j in up]
    last = stacked[:, :, length - halo :]
    first = stacked[:, :, :halo]
    last = last.at[1, :, 0].set(alive_float)
    first = first.at[1, :, halo - 1].set(alive_float)
    before = lax.ppermute(last, "gy", up)
    after = lax.ppermute(first, "gy", down)
    stacked = jnp.concatenate([before, stacked, after], axis=2)
    level_ext = stacked[0]
    speed_one = stacked[1:4, :, SPAN:-SPAN]
    speed_two = speed_one[:, :, SPAN:-SPAN]
    speed_three = speed_two[:, :, SPAN:-SPAN]
    ring_width = length + 2
    place = lax.broadcasted_iota(jnp.int32, (1, ring_width, 1), 1)
    flag_ring = jnp.where(
        place == 0,
        before[1, 0, 0, 0],
        jnp.where(place == ring_width - 1, after[1, 0, halo - 1, 0], alive_float),
    )

    inner, rate = stage_rate(level_ext, speed_one)
    section_one = inner + time_step * rate
    inner, rate = stage_rate(section_one, speed_two)
    section_two = 0.75 * level_ext[:, 2 * SPAN : -2 * SPAN] + 0.25 * (inner + time_step * rate)
    inner, rate = stage_rate(section_two, speed_three)
    level_ring = level_ext[:, 3 * SPAN : -3 * SPAN]
    advanced = level_ring / 3.0 + 2.0 / 3.0 * (inner + time_step * rate)
    ringed = jnp.where(flag_ring > 0, advanced, level_ring)
    level_out = ringed[:, 1:-1]
    rim = x_faces(ringed, 1)

    group = lax.axis_size("gz")
    ascending = depth_order[0] < depth_order[group - 1]
    left_x = 0.75 * rim[1:-1] + 0.25 * rim[:-2]
    right_x = 0.75 * rim[1:-1] + 0.25 * rim[2:]
    grid_pairs = []
    for along_x in (left_x, right_x):
        pair_list = []
        for neighbour in (along_x[:, :-2], along_x[:, 2:]):
            samples = 0.75 * along_x[:, 1:-1] + 0.25 * neighbour
            pair_list.append(shade(samples, alive_float, ascending))
        grid_pairs.append(pair_list)
    slab_image = alternate(grid_pairs)
    rows_each = slab_image.shape[1] // group
    columns = slab_image.shape[2]
    pieces = slab_image.reshape(4, group, rows_each, columns)
    received = lax.all_to_all(pieces, "gz", split_axis=1, concat_axis=1, tiled=True)
    blended = jnp.concatenate(
        [
            jnp.zeros((3, rows_each, columns), jnp.float32),
            jnp.ones((1, rows_each, columns), jnp.float32),
        ],
        0,
    )
    for rank_value in range(group):
        chooser = (depth_order == rank_value).astype(jnp.float32)
        piece_now = jnp.einsum("s,csij->cij", chooser, received, precision=lax.Precision.HIGHEST)
        blended = over(blended, piece_now)
    image = jnp.concatenate([blended[:3], 1.0 - blended[3:]], 0)
    return (level_out, image)


def solution(mesh):
    placed = (P("gx", "gy", "gz"), P(None, "gx", "gy", "gz"), P("gx", "gy", "gz"), P())
    return jax.shard_map(
        shards,
        mesh=mesh,
        in_specs=placed,
        out_specs=(P("gx", "gy", "gz"), P(None, ("gx", "gz"), "gy")),
        check_vma=False,
    )
```

```python
import jax
import jax.numpy as jnp
from jax import lax
from jax.sharding import PartitionSpec as P

CZ = 128


time_step = 0.4
weno_floor = 1e-06
SPAN = 3


def exchange(fields, axis, widths, dim):
    size = lax.axis_size(axis)
    up = [(i, (i + 1) % size) for i in range(size)]
    down = [(j, i) for i, j in up]
    out = []
    for field, w in zip(fields, widths):
        d = dim + field.ndim - 3
        last = lax.slice_in_dim(field, field.shape[d] - w, field.shape[d], axis=d)
        first = lax.slice_in_dim(field, 0, w, axis=d)
        before = lax.ppermute(last, axis, up)
        after = lax.ppermute(first, axis, down)
        out.append(jnp.concatenate([before, field, after], axis=d))
    return out


def exchange_packed(fields, axis, widths):
    size = lax.axis_size(axis)
    up = [(i, (i + 1) % size) for i in range(size)]
    down = [(j, i) for i, j in up]
    dims = [field.ndim - 3 for field in fields]
    lasts = [
        lax.slice_in_dim(field, field.shape[d] - w, field.shape[d], axis=d)
        for field, w, d in zip(fields, widths, dims)
    ]
    firsts = [lax.slice_in_dim(field, 0, w, axis=d) for field, w, d in zip(fields, widths, dims)]

    def pack(parts):
        return jnp.concatenate([part.reshape(-1, part.shape[-1]) for part in parts], 0)

    def unpack(flat, like):
        out, at = [], 0
        for part in like:
            rows = part.size // part.shape[-1]
            out.append(flat[at : at + rows].reshape(part.shape))
            at += rows
        return out

    before = unpack(lax.ppermute(pack(lasts), axis, up), lasts)
    after = unpack(lax.ppermute(pack(firsts), axis, down), firsts)
    return [
        jnp.concatenate([b, field, a], axis=d)
        for b, field, a, d in zip(before, fields, after, dims)
    ]


def z_faces(x):
    size, length = (lax.axis_size("gz"), x.shape[2])
    up = [(i, (i + 1) % size) for i in range(size)]
    down = [(j, i) for i, j in up]
    before = lax.ppermute(x[:, :, length - SPAN :], "gz", up)
    after = lax.ppermute(x[:, :, :SPAN], "gz", down)
    return jnp.concatenate([before, x, after], axis=2)


def square(operand):
    return operand * operand


def weno_value(diff_one, diff_two, diff_three, diff_four, diff_five):
    candidate_one = diff_one / 3.0 - 7.0 * diff_two / 6.0 + 11.0 * diff_three / 6.0
    candidate_two = -diff_two / 6.0 + 5.0 * diff_three / 6.0 + diff_four / 3.0
    candidate_three = diff_three / 3.0 + 5.0 * diff_four / 6.0 - diff_five / 6.0
    smooth_one = 13.0 / 12.0 * square(diff_one - 2.0 * diff_two + diff_three) + 0.25 * square(
        diff_one - 4.0 * diff_two + 3.0 * diff_three
    )
    smooth_two = 13.0 / 12.0 * square(diff_two - 2.0 * diff_three + diff_four) + 0.25 * square(
        diff_two - diff_four
    )
    smooth_three = 13.0 / 12.0 * square(diff_three - 2.0 * diff_four + diff_five) + 0.25 * square(
        3.0 * diff_three - 4.0 * diff_four + diff_five
    )
    weight_one = 0.1 / square(weno_floor + smooth_one)
    weight_two = 0.6 / square(weno_floor + smooth_two)
    weight_three = 0.3 / square(weno_floor + smooth_three)
    return (
        weight_one * candidate_one + weight_two * candidate_two + weight_three * candidate_three
    ) / (weight_one + weight_two + weight_three)


def window(padded, axis_dim, offset):
    length = padded.shape[axis_dim] - 2 * SPAN
    return lax.slice_in_dim(padded, SPAN + offset, SPAN + offset + length, axis=axis_dim)


def local_rate(padded_list, speeds):
    summed = jnp.zeros(speeds.shape[1:], jnp.float32)
    for axis_dim in range(3):
        padded = padded_list[axis_dim]
        jump_list = [
            window(padded, axis_dim, offset) - window(padded, axis_dim, offset - 1)
            for offset in range(-2, 4)
        ]
        from_left = weno_value(jump_list[0], jump_list[1], jump_list[2], jump_list[3], jump_list[4])
        from_right = weno_value(
            jump_list[5], jump_list[4], jump_list[3], jump_list[2], jump_list[1]
        )
        speed_axis = speeds[axis_dim]
        summed = (
            summed
            + jnp.maximum(speed_axis, 0.0) * from_left
            + jnp.minimum(speed_axis, 0.0) * from_right
        )
    return -summed


def shade(samples, alive, ascending):
    opacity = alive * (2.0 / CZ) / (1.0 + 4.0 * samples * samples)
    log_clear = jnp.log1p(-opacity)
    depth = jnp.arange(CZ)
    ahead = jnp.where(
        ascending, depth[:, None] < depth[None, :], depth[:, None] > depth[None, :]
    ).astype(jnp.float32)
    flat_logs = log_clear.reshape(-1, CZ)
    before = jnp.dot(flat_logs, ahead, precision=lax.Precision.HIGHEST).reshape(log_clear.shape)
    weight = jnp.exp(before) * opacity
    bright = jnp.tanh(samples)
    red = jnp.sum(weight * (0.5 + 0.5 * bright), -1)
    green = jnp.sum(weight * (0.5 - 0.5 * bright), -1)
    blue = jnp.sum(weight / (1.0 + samples * samples), -1)
    clear = jnp.exp(jnp.sum(log_clear, -1))
    return jnp.stack([red, green, blue, clear])


def alternate(grid_pairs):
    row_list = [jnp.stack(pixel_pair, -1) for pixel_pair in grid_pairs]
    joined = jnp.stack(row_list, -3)
    joined_shape = joined.shape
    return joined.reshape(joined_shape[:-4] + (joined_shape[-4] * 2, joined_shape[-2] * 2))


def over(front_part, back_part):
    colour = front_part[:3] + front_part[3:] * back_part[:3]
    clear = front_part[3:] * back_part[3:]
    return jnp.concatenate([colour, clear], 0)


def x_faces(x, width):
    size, length = (lax.axis_size("gx"), x.shape[0])
    up = [(i, (i + 1) % size) for i in range(size)]
    down = [(j, i) for i, j in up]
    before = lax.ppermute(x[length - width :], "gx", up)
    after = lax.ppermute(x[:width], "gx", down)
    return jnp.concatenate([before, x, after], axis=0)


def stage_rate(field, speeds):
    inner = field[:, SPAN:-SPAN]
    padded = [x_faces(inner, SPAN), field, z_faces(inner)]
    return inner, local_rate(padded, speeds)


def shards(level_set, velocity, active_brick, depth_order):
    alive = active_brick[0, 0, 0] > 0
    alive_float = alive.astype(jnp.float32)
    flags = jnp.broadcast_to(alive_float, level_set.shape)
    stacked = jnp.stack([level_set] + [velocity[d].astype(jnp.float32) for d in range(3)] + [flags])
    halo = 3 * SPAN + 1
    stacked = exchange([stacked], "gy", [halo], 1)[0]
    level_ext = stacked[0]
    carried = stacked[1:5, :, SPAN:-SPAN]
    speed_one = carried[:3]
    speed_two = speed_one[:, :, SPAN:-SPAN]
    flag_ring = stacked[4, :, 3 * SPAN : -3 * SPAN]

    size = lax.axis_size("gx")
    up = [(i, (i + 1) % size) for i in range(size)]
    down = [(j, i) for i, j in up]
    inner = level_ext[:, SPAN:-SPAN]
    last = jnp.concatenate([inner[-SPAN:]] + [carried[c, -1:] for c in range(4)], 0)
    first = jnp.concatenate([inner[:SPAN]] + [carried[c, :1] for c in range(4)], 0)
    before = lax.ppermute(last, "gx", up)
    after = lax.ppermute(first, "gx", down)
    padded = [
        jnp.concatenate([before[:SPAN], inner, after[:SPAN]], 0),
        level_ext,
        z_faces(inner),
    ]
    section_one = inner + time_step * local_rate(padded, speed_one)
    inner, rate = stage_rate(section_one, speed_two)
    section_two = 0.75 * level_ext[:, 2 * SPAN : -2 * SPAN] + 0.25 * (inner + time_step * rate)

    ring = slice(2 * SPAN, -2 * SPAN)
    edge_before = before[SPAN - 1 :, ring]
    edge_after = jnp.concatenate([after[:1], after[SPAN:]], 0)[:, ring]
    wide = x_faces(section_two, SPAN + 1)
    inner = wide[SPAN:-SPAN, SPAN:-SPAN]
    across, along, depth = wide[:, SPAN:-SPAN], wide[SPAN:-SPAN], z_faces(inner)
    rows = inner.shape[0]

    def part(lo, hi, speeds, level, flag):
        padded = [across[lo : hi + 2 * SPAN], along[lo:hi], depth[lo:hi]]
        rate = local_rate(padded, speeds)
        advanced = level / 3.0 + 2.0 / 3.0 * (inner[lo:hi] + time_step * rate)
        return jnp.where(flag > 0, advanced, level)

    rim = jnp.concatenate(
        [
            part(0, 1, edge_before[1:4][:, None], edge_before[:1], edge_before[4:5]),
            part(
                1,
                rows - 1,
                speed_two[:, :, SPAN:-SPAN],
                level_ext[:, 3 * SPAN : -3 * SPAN],
                flag_ring,
            ),
            part(rows - 1, rows, edge_after[1:4][:, None], edge_after[:1], edge_after[4:5]),
        ],
        0,
    )
    level_out = rim[1:-1, 1:-1]

    group = lax.axis_size("gz")
    ascending = depth_order[0] < depth_order[group - 1]
    left_x = 0.75 * rim[1:-1] + 0.25 * rim[:-2]
    right_x = 0.75 * rim[1:-1] + 0.25 * rim[2:]
    grid_pairs = []
    for along_x in (left_x, right_x):
        pair_list = []
        for neighbour in (along_x[:, :-2], along_x[:, 2:]):
            samples = 0.75 * along_x[:, 1:-1] + 0.25 * neighbour
            pair_list.append(shade(samples, alive_float, ascending))
        grid_pairs.append(pair_list)
    slab_image = alternate(grid_pairs)
    rows_each = slab_image.shape[1] // group
    columns = slab_image.shape[2]
    pieces = slab_image.reshape(4, group, rows_each, columns)
    received = lax.all_to_all(pieces, "gz", split_axis=1, concat_axis=1, tiled=True)
    blended = jnp.concatenate(
        [
            jnp.zeros((3, rows_each, columns), jnp.float32),
            jnp.ones((1, rows_each, columns), jnp.float32),
        ],
        0,
    )
    for rank_value in range(group):
        chooser = (depth_order == rank_value).astype(jnp.float32)
        piece_now = jnp.einsum("s,csij->cij", chooser, received, precision=lax.Precision.HIGHEST)
        blended = over(blended, piece_now)
    image = jnp.concatenate([blended[:3], 1.0 - blended[3:]], 0)
    return (level_out, image)


def solution(mesh):
    placed = (P("gx", "gy", "gz"), P(None, "gx", "gy", "gz"), P("gx", "gy", "gz"), P())
    return jax.shard_map(
        shards,
        mesh=mesh,
        in_specs=placed,
        out_specs=(P("gx", "gy", "gz"), P(None, ("gx", "gz"), "gy")),
        check_vma=False,
    )
```

```python
import jax
import jax.numpy as jnp
from jax import lax
from jax.sharding import PartitionSpec as P

CZ = 128


time_step = 0.4
weno_floor = 1e-06
SPAN = 3


def exchange(fields, axis, widths, dim):
    size = lax.axis_size(axis)
    up = [(i, (i + 1) % size) for i in range(size)]
    down = [(j, i) for i, j in up]
    out = []
    for field, w in zip(fields, widths):
        d = dim + field.ndim - 3
        last = lax.slice_in_dim(field, field.shape[d] - w, field.shape[d], axis=d)
        first = lax.slice_in_dim(field, 0, w, axis=d)
        before = lax.ppermute(last, axis, up)
        after = lax.ppermute(first, axis, down)
        out.append(jnp.concatenate([before, field, after], axis=d))
    return out


def exchange_packed(fields, axis, widths):
    size = lax.axis_size(axis)
    up = [(i, (i + 1) % size) for i in range(size)]
    down = [(j, i) for i, j in up]
    dims = [field.ndim - 3 for field in fields]
    lasts = [
        lax.slice_in_dim(field, field.shape[d] - w, field.shape[d], axis=d)
        for field, w, d in zip(fields, widths, dims)
    ]
    firsts = [lax.slice_in_dim(field, 0, w, axis=d) for field, w, d in zip(fields, widths, dims)]

    def pack(parts):
        return jnp.concatenate([part.reshape(-1, part.shape[-1]) for part in parts], 0)

    def unpack(flat, like):
        out, at = [], 0
        for part in like:
            rows = part.size // part.shape[-1]
            out.append(flat[at : at + rows].reshape(part.shape))
            at += rows
        return out

    before = unpack(lax.ppermute(pack(lasts), axis, up), lasts)
    after = unpack(lax.ppermute(pack(firsts), axis, down), firsts)
    return [
        jnp.concatenate([b, field, a], axis=d)
        for b, field, a, d in zip(before, fields, after, dims)
    ]


def z_faces(x):
    size, length = (lax.axis_size("gz"), x.shape[2])
    up = [(i, (i + 1) % size) for i in range(size)]
    down = [(j, i) for i, j in up]
    before = lax.ppermute(x[:, :, length - SPAN :], "gz", up)
    after = lax.ppermute(x[:, :, :SPAN], "gz", down)
    return jnp.concatenate([before, x, after], axis=2)


def square(operand):
    return operand * operand


def weno_value(diff_one, diff_two, diff_three, diff_four, diff_five):
    candidate_one = diff_one / 3.0 - 7.0 * diff_two / 6.0 + 11.0 * diff_three / 6.0
    candidate_two = -diff_two / 6.0 + 5.0 * diff_three / 6.0 + diff_four / 3.0
    candidate_three = diff_three / 3.0 + 5.0 * diff_four / 6.0 - diff_five / 6.0
    smooth_one = 13.0 / 12.0 * square(diff_one - 2.0 * diff_two + diff_three) + 0.25 * square(
        diff_one - 4.0 * diff_two + 3.0 * diff_three
    )
    smooth_two = 13.0 / 12.0 * square(diff_two - 2.0 * diff_three + diff_four) + 0.25 * square(
        diff_two - diff_four
    )
    smooth_three = 13.0 / 12.0 * square(diff_three - 2.0 * diff_four + diff_five) + 0.25 * square(
        3.0 * diff_three - 4.0 * diff_four + diff_five
    )
    weight_one = 0.1 / square(weno_floor + smooth_one)
    weight_two = 0.6 / square(weno_floor + smooth_two)
    weight_three = 0.3 / square(weno_floor + smooth_three)
    return (
        weight_one * candidate_one + weight_two * candidate_two + weight_three * candidate_three
    ) / (weight_one + weight_two + weight_three)


def window(padded, axis_dim, offset):
    length = padded.shape[axis_dim] - 2 * SPAN
    return lax.slice_in_dim(padded, SPAN + offset, SPAN + offset + length, axis=axis_dim)


def local_rate(padded_list, speeds):
    summed = jnp.zeros(speeds.shape[1:], jnp.float32)
    for axis_dim in range(3):
        padded = padded_list[axis_dim]
        jump_list = [
            window(padded, axis_dim, offset) - window(padded, axis_dim, offset - 1)
            for offset in range(-2, 4)
        ]
        from_left = weno_value(jump_list[0], jump_list[1], jump_list[2], jump_list[3], jump_list[4])
        from_right = weno_value(
            jump_list[5], jump_list[4], jump_list[3], jump_list[2], jump_list[1]
        )
        speed_axis = speeds[axis_dim]
        summed = (
            summed
            + jnp.maximum(speed_axis, 0.0) * from_left
            + jnp.minimum(speed_axis, 0.0) * from_right
        )
    return -summed


def shade(samples, alive, ascending):
    opacity = alive * (2.0 / CZ) / (1.0 + 4.0 * samples * samples)
    log_clear = jnp.log1p(-opacity)
    depth = jnp.arange(CZ)
    ahead = jnp.where(
        ascending, depth[:, None] < depth[None, :], depth[:, None] > depth[None, :]
    ).astype(jnp.float32)
    flat_logs = log_clear.reshape(-1, CZ)
    before = jnp.dot(flat_logs, ahead, precision=lax.Precision.HIGHEST).reshape(log_clear.shape)
    weight = jnp.exp(before) * opacity
    bright = jnp.tanh(samples)
    red = jnp.sum(weight * (0.5 + 0.5 * bright), -1)
    green = jnp.sum(weight * (0.5 - 0.5 * bright), -1)
    blue = jnp.sum(weight / (1.0 + samples * samples), -1)
    clear = jnp.exp(jnp.sum(log_clear, -1))
    return jnp.stack([red, green, blue, clear])


def alternate(grid_pairs):
    row_list = [jnp.stack(pixel_pair, -1) for pixel_pair in grid_pairs]
    joined = jnp.stack(row_list, -3)
    joined_shape = joined.shape
    return joined.reshape(joined_shape[:-4] + (joined_shape[-4] * 2, joined_shape[-2] * 2))


def over(front_part, back_part):
    colour = front_part[:3] + front_part[3:] * back_part[:3]
    clear = front_part[3:] * back_part[3:]
    return jnp.concatenate([colour, clear], 0)


def x_faces(x, width):
    size, length = (lax.axis_size("gx"), x.shape[0])
    up = [(i, (i + 1) % size) for i in range(size)]
    down = [(j, i) for i, j in up]
    before = lax.ppermute(x[length - width :], "gx", up)
    after = lax.ppermute(x[:width], "gx", down)
    return jnp.concatenate([before, x, after], axis=0)


def stage_rate(field, speeds):
    inner = field[:, SPAN:-SPAN]
    padded = [x_faces(inner, SPAN), field, z_faces(inner)]
    return inner, local_rate(padded, speeds)


def shards(level_set, velocity, active_brick, depth_order):
    alive = active_brick[0, 0, 0] > 0
    alive_float = alive.astype(jnp.float32)
    stacked = jnp.stack([level_set] + [velocity[d].astype(jnp.float32) for d in range(3)])
    halo = 3 * SPAN + 1
    size, length = (lax.axis_size("gy"), stacked.shape[2])
    up = [(i, (i + 1) % size) for i in range(size)]
    down = [(j, i) for i, j in up]
    last = stacked[:, :, length - halo :].at[1, :, 0].set(alive_float)
    first = stacked[:, :, :halo].at[1, :, halo - 1].set(alive_float)
    y_before = lax.ppermute(last, "gy", up)
    y_after = lax.ppermute(first, "gy", down)
    stacked = jnp.concatenate([y_before, stacked, y_after], axis=2)
    flag_low, flag_high = y_before[1, 0, 0, 0], y_after[1, 0, halo - 1, 0]

    def flag_column(width):
        place = lax.broadcasted_iota(jnp.int32, (1, length + 2 * width, 1), 1)
        low = jnp.where(place < width, flag_low, alive_float)
        return jnp.where(place >= length + width, flag_high, low)

    level_ext = stacked[0]
    speed_one = stacked[1:4, :, SPAN:-SPAN]
    speed_two = speed_one[:, :, SPAN:-SPAN]
    flag_ring = flag_column(1)

    size = lax.axis_size("gx")
    up = [(i, (i + 1) % size) for i in range(size)]
    down = [(j, i) for i, j in up]
    inner = level_ext[:, SPAN:-SPAN]
    flag_row = jnp.broadcast_to(flag_column(halo - SPAN), (1,) + inner.shape[1:])
    last = jnp.concatenate([inner[-SPAN:]] + [speed_one[c, -1:] for c in range(3)] + [flag_row], 0)
    first = jnp.concatenate([inner[:SPAN]] + [speed_one[c, :1] for c in range(3)] + [flag_row], 0)
    before = lax.ppermute(last, "gx", up)
    after = lax.ppermute(first, "gx", down)
    padded = [
        jnp.concatenate([before[:SPAN], inner, after[:SPAN]], 0),
        level_ext,
        z_faces(inner),
    ]
    section_one = inner + time_step * local_rate(padded, speed_one)
    inner, rate = stage_rate(section_one, speed_two)
    section_two = 0.75 * level_ext[:, 2 * SPAN : -2 * SPAN] + 0.25 * (inner + time_step * rate)

    ring = slice(2 * SPAN, -2 * SPAN)
    edge_before = before[SPAN - 1 :, ring]
    edge_after = jnp.concatenate([after[:1], after[SPAN:]], 0)[:, ring]
    wide = x_faces(section_two, SPAN + 1)
    inner = wide[SPAN:-SPAN, SPAN:-SPAN]
    across, along, depth = wide[:, SPAN:-SPAN], wide[SPAN:-SPAN], z_faces(inner)
    rows = inner.shape[0]

    def part(lo, hi, speeds, level, flag):
        padded = [across[lo : hi + 2 * SPAN], along[lo:hi], depth[lo:hi]]
        rate = local_rate(padded, speeds)
        advanced = level / 3.0 + 2.0 / 3.0 * (inner[lo:hi] + time_step * rate)
        return jnp.where(flag > 0, advanced, level)

    rim = jnp.concatenate(
        [
            part(0, 1, edge_before[1:4][:, None], edge_before[:1], edge_before[4:5]),
            part(
                1,
                rows - 1,
                speed_two[:, :, SPAN:-SPAN],
                level_ext[:, 3 * SPAN : -3 * SPAN],
                flag_ring,
            ),
            part(rows - 1, rows, edge_after[1:4][:, None], edge_after[:1], edge_after[4:5]),
        ],
        0,
    )
    level_out = rim[1:-1, 1:-1]

    group = lax.axis_size("gz")
    ascending = depth_order[0] < depth_order[group - 1]
    left_x = 0.75 * rim[1:-1] + 0.25 * rim[:-2]
    right_x = 0.75 * rim[1:-1] + 0.25 * rim[2:]
    grid_pairs = []
    for along_x in (left_x, right_x):
        pair_list = []
        for neighbour in (along_x[:, :-2], along_x[:, 2:]):
            samples = 0.75 * along_x[:, 1:-1] + 0.25 * neighbour
            pair_list.append(shade(samples, alive_float, ascending))
        grid_pairs.append(pair_list)
    slab_image = alternate(grid_pairs)
    rows_each = slab_image.shape[1] // group
    columns = slab_image.shape[2]
    pieces = slab_image.reshape(4, group, rows_each, columns)
    received = lax.all_to_all(pieces, "gz", split_axis=1, concat_axis=1, tiled=True)
    blended = jnp.concatenate(
        [
            jnp.zeros((3, rows_each, columns), jnp.float32),
            jnp.ones((1, rows_each, columns), jnp.float32),
        ],
        0,
    )
    for rank_value in range(group):
        chooser = (depth_order == rank_value).astype(jnp.float32)
        piece_now = jnp.einsum("s,csij->cij", chooser, received, precision=lax.Precision.HIGHEST)
        blended = over(blended, piece_now)
    image = jnp.concatenate([blended[:3], 1.0 - blended[3:]], 0)
    return (level_out, image)


def solution(mesh):
    placed = (P("gx", "gy", "gz"), P(None, "gx", "gy", "gz"), P("gx", "gy", "gz"), P())
    return jax.shard_map(
        shards,
        mesh=mesh,
        in_specs=placed,
        out_specs=(P("gx", "gy", "gz"), P(None, ("gx", "gz"), "gy")),
        check_vma=False,
    )
```

```python
import jax
import jax.numpy as jnp
from jax import lax
from jax.sharding import PartitionSpec as P

CZ = 128


time_step = 0.4
weno_floor = 1e-06
SPAN = 3


def exchange(fields, axis, widths, dim):
    size = lax.axis_size(axis)
    up = [(i, (i + 1) % size) for i in range(size)]
    down = [(j, i) for i, j in up]
    out = []
    for field, w in zip(fields, widths):
        d = dim + field.ndim - 3
        last = lax.slice_in_dim(field, field.shape[d] - w, field.shape[d], axis=d)
        first = lax.slice_in_dim(field, 0, w, axis=d)
        before = lax.ppermute(last, axis, up)
        after = lax.ppermute(first, axis, down)
        out.append(jnp.concatenate([before, field, after], axis=d))
    return out


def exchange_packed(fields, axis, widths):
    size = lax.axis_size(axis)
    up = [(i, (i + 1) % size) for i in range(size)]
    down = [(j, i) for i, j in up]
    dims = [field.ndim - 3 for field in fields]
    lasts = [
        lax.slice_in_dim(field, field.shape[d] - w, field.shape[d], axis=d)
        for field, w, d in zip(fields, widths, dims)
    ]
    firsts = [lax.slice_in_dim(field, 0, w, axis=d) for field, w, d in zip(fields, widths, dims)]

    def pack(parts):
        return jnp.concatenate([part.reshape(-1, part.shape[-1]) for part in parts], 0)

    def unpack(flat, like):
        out, at = [], 0
        for part in like:
            rows = part.size // part.shape[-1]
            out.append(flat[at : at + rows].reshape(part.shape))
            at += rows
        return out

    before = unpack(lax.ppermute(pack(lasts), axis, up), lasts)
    after = unpack(lax.ppermute(pack(firsts), axis, down), firsts)
    return [
        jnp.concatenate([b, field, a], axis=d)
        for b, field, a, d in zip(before, fields, after, dims)
    ]


def z_faces(x):
    size, length = (lax.axis_size("gz"), x.shape[2])
    up = [(i, (i + 1) % size) for i in range(size)]
    down = [(j, i) for i, j in up]
    before = lax.ppermute(x[:, :, length - SPAN :], "gz", up)
    after = lax.ppermute(x[:, :, :SPAN], "gz", down)
    return jnp.concatenate([before, x, after], axis=2)


def square(operand):
    return operand * operand


def weno_value(diff_one, diff_two, diff_three, diff_four, diff_five):
    candidate_one = diff_one / 3.0 - 7.0 * diff_two / 6.0 + 11.0 * diff_three / 6.0
    candidate_two = -diff_two / 6.0 + 5.0 * diff_three / 6.0 + diff_four / 3.0
    candidate_three = diff_three / 3.0 + 5.0 * diff_four / 6.0 - diff_five / 6.0
    smooth_one = 13.0 / 12.0 * square(diff_one - 2.0 * diff_two + diff_three) + 0.25 * square(
        diff_one - 4.0 * diff_two + 3.0 * diff_three
    )
    smooth_two = 13.0 / 12.0 * square(diff_two - 2.0 * diff_three + diff_four) + 0.25 * square(
        diff_two - diff_four
    )
    smooth_three = 13.0 / 12.0 * square(diff_three - 2.0 * diff_four + diff_five) + 0.25 * square(
        3.0 * diff_three - 4.0 * diff_four + diff_five
    )
    weight_one = 0.1 / square(weno_floor + smooth_one)
    weight_two = 0.6 / square(weno_floor + smooth_two)
    weight_three = 0.3 / square(weno_floor + smooth_three)
    return (
        weight_one * candidate_one + weight_two * candidate_two + weight_three * candidate_three
    ) / (weight_one + weight_two + weight_three)


def window(padded, axis_dim, offset):
    length = padded.shape[axis_dim] - 2 * SPAN
    return lax.slice_in_dim(padded, SPAN + offset, SPAN + offset + length, axis=axis_dim)


def local_rate(padded_list, speeds):
    summed = jnp.zeros(speeds.shape[1:], jnp.float32)
    for axis_dim in range(3):
        padded = padded_list[axis_dim]
        jump_list = [
            window(padded, axis_dim, offset) - window(padded, axis_dim, offset - 1)
            for offset in range(-2, 4)
        ]
        from_left = weno_value(jump_list[0], jump_list[1], jump_list[2], jump_list[3], jump_list[4])
        from_right = weno_value(
            jump_list[5], jump_list[4], jump_list[3], jump_list[2], jump_list[1]
        )
        speed_axis = speeds[axis_dim]
        summed = (
            summed
            + jnp.maximum(speed_axis, 0.0) * from_left
            + jnp.minimum(speed_axis, 0.0) * from_right
        )
    return -summed


def shade(samples, alive, ascending):
    opacity = alive * (2.0 / CZ) / (1.0 + 4.0 * samples * samples)
    log_clear = jnp.log1p(-opacity)
    depth = jnp.arange(CZ)
    ahead = jnp.where(
        ascending, depth[:, None] < depth[None, :], depth[:, None] > depth[None, :]
    ).astype(jnp.float32)
    flat_logs = log_clear.reshape(-1, CZ)
    before = jnp.dot(flat_logs, ahead, precision=lax.Precision.HIGHEST).reshape(log_clear.shape)
    weight = jnp.exp(before) * opacity
    bright = jnp.tanh(samples)
    red = jnp.sum(weight * (0.5 + 0.5 * bright), -1)
    green = jnp.sum(weight * (0.5 - 0.5 * bright), -1)
    blue = jnp.sum(weight / (1.0 + samples * samples), -1)
    clear = jnp.exp(jnp.sum(log_clear, -1))
    return jnp.stack([red, green, blue, clear])


def alternate(grid_pairs):
    row_list = [jnp.stack(pixel_pair, -1) for pixel_pair in grid_pairs]
    joined = jnp.stack(row_list, -3)
    joined_shape = joined.shape
    return joined.reshape(joined_shape[:-4] + (joined_shape[-4] * 2, joined_shape[-2] * 2))


def over(front_part, back_part):
    colour = front_part[:3] + front_part[3:] * back_part[:3]
    clear = front_part[3:] * back_part[3:]
    return jnp.concatenate([colour, clear], 0)


def x_faces(x, width):
    size, length = (lax.axis_size("gx"), x.shape[0])
    up = [(i, (i + 1) % size) for i in range(size)]
    down = [(j, i) for i, j in up]
    before = lax.ppermute(x[length - width :], "gx", up)
    after = lax.ppermute(x[:width], "gx", down)
    return jnp.concatenate([before, x, after], axis=0)


def stage_rate(field, speeds):
    inner = field[:, SPAN:-SPAN]
    padded = [x_faces(inner, SPAN), field, z_faces(inner)]
    return inner, local_rate(padded, speeds)


def shards(level_set, velocity, active_brick, depth_order):
    alive = active_brick[0, 0, 0] > 0
    alive_float = alive.astype(jnp.float32)
    flags = jnp.broadcast_to(alive_float, level_set.shape)
    stacked = jnp.stack([level_set] + [velocity[d].astype(jnp.float32) for d in range(3)] + [flags])
    halo = 3 * SPAN + 1
    stacked = exchange([stacked], "gy", [halo], 1)[0]
    level_ext = stacked[0]
    carried = stacked[1:5, :, SPAN:-SPAN]
    speed_one = carried[:3]
    speed_two = speed_one[:, :, SPAN:-SPAN]
    flag_ring = stacked[4, :, 3 * SPAN : -3 * SPAN]

    size = lax.axis_size("gx")
    up = [(i, (i + 1) % size) for i in range(size)]
    down = [(j, i) for i, j in up]
    inner = level_ext[:, SPAN:-SPAN]
    last = jnp.concatenate([inner[-SPAN:]] + [carried[c, -1:] for c in range(4)], 0)
    first = jnp.concatenate([inner[:SPAN]] + [carried[c, :1] for c in range(4)], 0)
    before = lax.ppermute(last, "gx", up)
    after = lax.ppermute(first, "gx", down)
    padded = [
        jnp.concatenate([before[:SPAN], inner, after[:SPAN]], 0),
        level_ext,
        z_faces(inner),
    ]
    section_one = inner + time_step * local_rate(padded, speed_one)
    inner, rate = stage_rate(section_one, speed_two)
    section_two = 0.75 * level_ext[:, 2 * SPAN : -2 * SPAN] + 0.25 * (inner + time_step * rate)

    ring = slice(2 * SPAN, -2 * SPAN)
    edge_before = before[SPAN - 1 :, ring]
    edge_after = jnp.concatenate([after[:1], after[SPAN:]], 0)[:, ring]
    wide = x_faces(section_two, SPAN + 1)
    inner = wide[SPAN:-SPAN, SPAN:-SPAN]
    across, along, depth = wide[:, SPAN:-SPAN], wide[SPAN:-SPAN], z_faces(inner)
    rows = inner.shape[0]

    def part(lo, hi, speeds, level, flag):
        padded = [across[lo : hi + 2 * SPAN], along[lo:hi], depth[lo:hi]]
        rate = local_rate(padded, speeds)
        advanced = level / 3.0 + 2.0 / 3.0 * (inner[lo:hi] + time_step * rate)
        return jnp.where(flag > 0, advanced, level)

    rim = jnp.concatenate(
        [
            part(0, 1, edge_before[1:4][:, None], edge_before[:1], edge_before[4:5]),
            part(
                1,
                rows - 1,
                speed_two[:, :, SPAN:-SPAN],
                level_ext[:, 3 * SPAN : -3 * SPAN],
                flag_ring,
            ),
            part(rows - 1, rows, edge_after[1:4][:, None], edge_after[:1], edge_after[4:5]),
        ],
        0,
    )
    level_out = rim[1:-1, 1:-1]

    group = lax.axis_size("gz")
    ascending = depth_order[0] < depth_order[group - 1]
    left_x = 0.75 * rim[1:-1] + 0.25 * rim[:-2]
    right_x = 0.75 * rim[1:-1] + 0.25 * rim[2:]
    grid_pairs = []
    for along_x in (left_x, right_x):
        pair_list = []
        for neighbour in (along_x[:, :-2], along_x[:, 2:]):
            samples = 0.75 * along_x[:, 1:-1] + 0.25 * neighbour
            pair_list.append(shade(samples, alive_float, ascending))
        grid_pairs.append(pair_list)
    slab_image = alternate(grid_pairs)
    rows_each = slab_image.shape[1] // group
    columns = slab_image.shape[2]
    pieces = slab_image.reshape(4, group, rows_each, columns)
    received = lax.all_to_all(pieces, "gz", split_axis=1, concat_axis=1, tiled=True)
    blended = jnp.concatenate(
        [
            jnp.zeros((3, rows_each, columns), jnp.float32),
            jnp.ones((1, rows_each, columns), jnp.float32),
        ],
        0,
    )
    for rank_value in range(group):
        slab_index = jnp.sum(jnp.where(depth_order == rank_value, jnp.arange(group), 0))
        piece_now = lax.dynamic_index_in_dim(received, slab_index, axis=1, keepdims=False)
        blended = over(blended, piece_now)
    image = jnp.concatenate([blended[:3], 1.0 - blended[3:]], 0)
    return (level_out, image)


def solution(mesh):
    placed = (P("gx", "gy", "gz"), P(None, "gx", "gy", "gz"), P("gx", "gy", "gz"), P())
    return jax.shard_map(
        shards,
        mesh=mesh,
        in_specs=placed,
        out_specs=(P("gx", "gy", "gz"), P(None, ("gx", "gz"), "gy")),
        check_vma=False,
    )
```

```python
import jax
import jax.numpy as jnp
from jax import lax
from jax.sharding import PartitionSpec as P

CZ = 128


time_step = 0.4
weno_floor = 1e-06
SPAN = 3


def exchange(fields, axis, widths, dim):
    size = lax.axis_size(axis)
    up = [(i, (i + 1) % size) for i in range(size)]
    down = [(j, i) for i, j in up]
    out = []
    for field, w in zip(fields, widths):
        d = dim + field.ndim - 3
        last = lax.slice_in_dim(field, field.shape[d] - w, field.shape[d], axis=d)
        first = lax.slice_in_dim(field, 0, w, axis=d)
        before = lax.ppermute(last, axis, up)
        after = lax.ppermute(first, axis, down)
        out.append(jnp.concatenate([before, field, after], axis=d))
    return out


def exchange_packed(fields, axis, widths):
    size = lax.axis_size(axis)
    up = [(i, (i + 1) % size) for i in range(size)]
    down = [(j, i) for i, j in up]
    dims = [field.ndim - 3 for field in fields]
    lasts = [
        lax.slice_in_dim(field, field.shape[d] - w, field.shape[d], axis=d)
        for field, w, d in zip(fields, widths, dims)
    ]
    firsts = [lax.slice_in_dim(field, 0, w, axis=d) for field, w, d in zip(fields, widths, dims)]

    def pack(parts):
        return jnp.concatenate([part.reshape(-1, part.shape[-1]) for part in parts], 0)

    def unpack(flat, like):
        out, at = [], 0
        for part in like:
            rows = part.size // part.shape[-1]
            out.append(flat[at : at + rows].reshape(part.shape))
            at += rows
        return out

    before = unpack(lax.ppermute(pack(lasts), axis, up), lasts)
    after = unpack(lax.ppermute(pack(firsts), axis, down), firsts)
    return [
        jnp.concatenate([b, field, a], axis=d)
        for b, field, a, d in zip(before, fields, after, dims)
    ]


def z_faces(x):
    size, length = (lax.axis_size("gz"), x.shape[2])
    up = [(i, (i + 1) % size) for i in range(size)]
    down = [(j, i) for i, j in up]
    before = lax.ppermute(x[:, :, length - SPAN :], "gz", up)
    after = lax.ppermute(x[:, :, :SPAN], "gz", down)
    return jnp.concatenate([before, x, after], axis=2)


def square(operand):
    return operand * operand


def weno_value(diff_one, diff_two, diff_three, diff_four, diff_five):
    candidate_one = diff_one / 3.0 - 7.0 * diff_two / 6.0 + 11.0 * diff_three / 6.0
    candidate_two = -diff_two / 6.0 + 5.0 * diff_three / 6.0 + diff_four / 3.0
    candidate_three = diff_three / 3.0 + 5.0 * diff_four / 6.0 - diff_five / 6.0
    smooth_one = 13.0 / 12.0 * square(diff_one - 2.0 * diff_two + diff_three) + 0.25 * square(
        diff_one - 4.0 * diff_two + 3.0 * diff_three
    )
    smooth_two = 13.0 / 12.0 * square(diff_two - 2.0 * diff_three + diff_four) + 0.25 * square(
        diff_two - diff_four
    )
    smooth_three = 13.0 / 12.0 * square(diff_three - 2.0 * diff_four + diff_five) + 0.25 * square(
        3.0 * diff_three - 4.0 * diff_four + diff_five
    )
    weight_one = 0.1 / square(weno_floor + smooth_one)
    weight_two = 0.6 / square(weno_floor + smooth_two)
    weight_three = 0.3 / square(weno_floor + smooth_three)
    return (
        weight_one * candidate_one + weight_two * candidate_two + weight_three * candidate_three
    ) / (weight_one + weight_two + weight_three)


def window(padded, axis_dim, offset):
    length = padded.shape[axis_dim] - 2 * SPAN
    return lax.slice_in_dim(padded, SPAN + offset, SPAN + offset + length, axis=axis_dim)


def local_rate(padded_list, speeds):
    summed = jnp.zeros(speeds.shape[1:], jnp.float32)
    for axis_dim in range(3):
        padded = padded_list[axis_dim]
        jump_list = [
            window(padded, axis_dim, offset) - window(padded, axis_dim, offset - 1)
            for offset in range(-2, 4)
        ]
        from_left = weno_value(jump_list[0], jump_list[1], jump_list[2], jump_list[3], jump_list[4])
        from_right = weno_value(
            jump_list[5], jump_list[4], jump_list[3], jump_list[2], jump_list[1]
        )
        speed_axis = speeds[axis_dim]
        summed = (
            summed
            + jnp.maximum(speed_axis, 0.0) * from_left
            + jnp.minimum(speed_axis, 0.0) * from_right
        )
    return -summed


def shade(samples, alive, ascending):
    opacity = alive * (2.0 / CZ) / (1.0 + 4.0 * samples * samples)
    log_clear = jnp.log1p(-opacity)
    depth = jnp.arange(CZ)
    ahead = jnp.where(
        ascending, depth[:, None] < depth[None, :], depth[:, None] > depth[None, :]
    ).astype(jnp.float32)
    flat_logs = log_clear.reshape(-1, CZ)
    before = jnp.dot(flat_logs, ahead, precision=lax.Precision.HIGH).reshape(log_clear.shape)
    weight = jnp.exp(before) * opacity
    bright = jnp.tanh(samples)
    red = jnp.sum(weight * (0.5 + 0.5 * bright), -1)
    green = jnp.sum(weight * (0.5 - 0.5 * bright), -1)
    blue = jnp.sum(weight / (1.0 + samples * samples), -1)
    clear = jnp.exp(jnp.sum(log_clear, -1))
    return jnp.stack([red, green, blue, clear])


def alternate(grid_pairs):
    row_list = [jnp.stack(pixel_pair, -1) for pixel_pair in grid_pairs]
    joined = jnp.stack(row_list, -3)
    joined_shape = joined.shape
    return joined.reshape(joined_shape[:-4] + (joined_shape[-4] * 2, joined_shape[-2] * 2))


def over(front_part, back_part):
    colour = front_part[:3] + front_part[3:] * back_part[:3]
    clear = front_part[3:] * back_part[3:]
    return jnp.concatenate([colour, clear], 0)


def x_faces(x, width):
    size, length = (lax.axis_size("gx"), x.shape[0])
    up = [(i, (i + 1) % size) for i in range(size)]
    down = [(j, i) for i, j in up]
    before = lax.ppermute(x[length - width :], "gx", up)
    after = lax.ppermute(x[:width], "gx", down)
    return jnp.concatenate([before, x, after], axis=0)


def stage_rate(field, speeds):
    inner = field[:, SPAN:-SPAN]
    padded = [x_faces(inner, SPAN), field, z_faces(inner)]
    return inner, local_rate(padded, speeds)


def shards(level_set, velocity, active_brick, depth_order):
    alive = active_brick[0, 0, 0] > 0
    alive_float = alive.astype(jnp.float32)
    flags = jnp.broadcast_to(alive_float, level_set.shape)
    stacked = jnp.stack([level_set] + [velocity[d].astype(jnp.float32) for d in range(3)] + [flags])
    halo = 3 * SPAN + 1
    stacked = exchange([stacked], "gy", [halo], 1)[0]
    level_ext = stacked[0]
    carried = stacked[1:5, :, SPAN:-SPAN]
    speed_one = carried[:3]
    speed_two = speed_one[:, :, SPAN:-SPAN]
    flag_ring = stacked[4, :, 3 * SPAN : -3 * SPAN]

    size = lax.axis_size("gx")
    up = [(i, (i + 1) % size) for i in range(size)]
    down = [(j, i) for i, j in up]
    inner = level_ext[:, SPAN:-SPAN]
    last = jnp.concatenate([inner[-SPAN:]] + [carried[c, -1:] for c in range(4)], 0)
    first = jnp.concatenate([inner[:SPAN]] + [carried[c, :1] for c in range(4)], 0)
    before = lax.ppermute(last, "gx", up)
    after = lax.ppermute(first, "gx", down)
    padded = [
        jnp.concatenate([before[:SPAN], inner, after[:SPAN]], 0),
        level_ext,
        z_faces(inner),
    ]
    section_one = inner + time_step * local_rate(padded, speed_one)
    inner, rate = stage_rate(section_one, speed_two)
    section_two = 0.75 * level_ext[:, 2 * SPAN : -2 * SPAN] + 0.25 * (inner + time_step * rate)

    ring = slice(2 * SPAN, -2 * SPAN)
    edge_before = before[SPAN - 1 :, ring]
    edge_after = jnp.concatenate([after[:1], after[SPAN:]], 0)[:, ring]
    wide = x_faces(section_two, SPAN + 1)
    inner = wide[SPAN:-SPAN, SPAN:-SPAN]
    across, along, depth = wide[:, SPAN:-SPAN], wide[SPAN:-SPAN], z_faces(inner)
    rows = inner.shape[0]

    def part(lo, hi, speeds, level, flag):
        padded = [across[lo : hi + 2 * SPAN], along[lo:hi], depth[lo:hi]]
        rate = local_rate(padded, speeds)
        advanced = level / 3.0 + 2.0 / 3.0 * (inner[lo:hi] + time_step * rate)
        return jnp.where(flag > 0, advanced, level)

    rim = jnp.concatenate(
        [
            part(0, 1, edge_before[1:4][:, None], edge_before[:1], edge_before[4:5]),
            part(
                1,
                rows - 1,
                speed_two[:, :, SPAN:-SPAN],
                level_ext[:, 3 * SPAN : -3 * SPAN],
                flag_ring,
            ),
            part(rows - 1, rows, edge_after[1:4][:, None], edge_after[:1], edge_after[4:5]),
        ],
        0,
    )
    level_out = rim[1:-1, 1:-1]

    group = lax.axis_size("gz")
    ascending = depth_order[0] < depth_order[group - 1]
    left_x = 0.75 * rim[1:-1] + 0.25 * rim[:-2]
    right_x = 0.75 * rim[1:-1] + 0.25 * rim[2:]
    grid_pairs = []
    for along_x in (left_x, right_x):
        pair_list = []
        for neighbour in (along_x[:, :-2], along_x[:, 2:]):
            samples = 0.75 * along_x[:, 1:-1] + 0.25 * neighbour
            pair_list.append(shade(samples, alive_float, ascending))
        grid_pairs.append(pair_list)
    slab_image = alternate(grid_pairs)
    rows_each = slab_image.shape[1] // group
    columns = slab_image.shape[2]
    pieces = slab_image.reshape(4, group, rows_each, columns)
    received = lax.all_to_all(pieces, "gz", split_axis=1, concat_axis=1, tiled=True)
    blended = jnp.concatenate(
        [
            jnp.zeros((3, rows_each, columns), jnp.float32),
            jnp.ones((1, rows_each, columns), jnp.float32),
        ],
        0,
    )
    for rank_value in range(group):
        chooser = (depth_order == rank_value).astype(jnp.float32)
        piece_now = jnp.einsum("s,csij->cij", chooser, received, precision=lax.Precision.HIGHEST)
        blended = over(blended, piece_now)
    image = jnp.concatenate([blended[:3], 1.0 - blended[3:]], 0)
    return (level_out, image)


def solution(mesh):
    placed = (P("gx", "gy", "gz"), P(None, "gx", "gy", "gz"), P("gx", "gy", "gz"), P())
    return jax.shard_map(
        shards,
        mesh=mesh,
        in_specs=placed,
        out_specs=(P("gx", "gy", "gz"), P(None, ("gx", "gz"), "gy")),
        check_vma=False,
    )
```
